128 devices in a mesh: group: 8 (over z, x_lo), req: 16 (over x_hi, y, core).
Axes of the slice: x: 4 (x_hi: 2, x_lo: 2; x = x_hi * 2 + x_lo), y: 4, z: 4, core: 2. Of those that a mesh axis runs over, the one named last changes fastest.
Arguments:
- layer_input: bfloat16 [16384, 3072], P(('group', 'req')), may hold values from -6 to 6
- queries: bfloat16 [16384, 3072], P(('group', 'req')), may hold values from -240 to 240, as said below
- suffix_kv: bfloat16 [16384, 2048], P(('group', 'req')), may hold values from -6 to 6
- past_kv: bfloat16 [32768, 2048], P(('group', 'req')), may hold values from -6 to 6
- prefix_kv: bfloat16 [2048, 2048], P(('group', 'req')), may hold values from -6 to 6
- suffix_len: int32 [128], P(('group', 'req')), may hold values from 1 to 128, 12288 in all
- past_len: int32 [128], P(('group', 'req')), may hold values from 1 to 256, 16384 in all
- out_weight: bfloat16 [3072, 3072], P('group'), may hold values from -0.109375 to 0.109375
- norm_gain: bfloat16 [3072], replicated, may hold values from 0.5 to 1.5
- gate_weight: bfloat16 [3072, 8192], P(None, 'req'), may hold values from -0.109375 to 0.109375
- up_weight: bfloat16 [3072, 8192], P(None, 'req'), may hold values from -0.109375 to 0.109375
- down_weight: bfloat16 [8192, 3072], P('req'), may hold values from -0.0625 to 0.0625
Outputs:
- layer_output: bfloat16 [16384, 3072], P(('group', 'req'))
The draws below stay inside these ranges and needn't reach their ends.
Inputs may be any that keep to these rules, and one draw needn't show every extreme that they name: `queries`: normally distributed entries; some rows may be far larger.
All inputs are finite; a program needn't handle non-finite values. No bound on the sum of `suffix_len` or of `past_len` on one device may be relied on, other than what follows from the above.
Results may differ from the reference program's by a relative error of at most 0.012.
Values may be sent and summed in bfloat16 or wider, within the bound.
No kernel may reach another device: no remote copies, remote signals or barrier semaphores. Data moves between devices by JAX's collectives and lax.ppermute only.
A program may use at most 128 MiB of HBM per device.

```python
import math
import jax
import jax.numpy as jnp
import numpy as np
from jax import lax

D = 3072
HEADS = 24
KV_HEADS = 8
HEAD = 128
FF = 8192
TOK_DEV = 128
PAST_DEV = 256
SINK = 4
QW = 3072
KVW = 2048
REQS = 128
TOKENS = 16384
PREFIX = 256
WINDOW = 384
N_GROUP = 8
N_REQ = 16


def draw_queries(key, part):
    values = jax.random.normal(key, (TOKENS, HEADS * HEAD), jnp.float32)
    values = jnp.clip(values, -6.0, 6.0)
    return values.astype(jnp.bfloat16)


def block_levels(own_key, extent, split, smallest, high):
    def one(position, blocks):
        draws = jax.random.uniform(jax.random.fold_in(jax.random.fold_in(own_key, 6), position), (blocks,), jnp.float32, smallest / len(split), high / len(split))
        return jnp.repeat(jnp.exp(draws), extent[position] // blocks).reshape((-1,) + (1,) * (len(extent) - position - 1))

    gain = one(*split[0])
    for cut in split[1:]:
        gain = gain * one(*cut)
    return gain


def length_profile(number_of, total, limit, skew):
    portions = [(1 << 20) // math.isqrt(grade ** skew) + 1 for grade in range(2, number_of + 1)]
    rest, counts = total - limit - (number_of - 1), [1] * (number_of - 1)
    while rest > 0:
        movable = [i for i in range(number_of - 1) if counts[i] < limit]
        whole, left = sum([portions[i] for i in movable]), rest
        for i in movable:
            more = min(limit - counts[i], max(1, left * portions[i] // whole), rest)
            counts[i] = counts[i] + more
            rest = rest - more
    return np.array([limit] + counts)


def uneven(key, count, total, limit, slope):
    if count == 2:
        one = jax.random.randint(key, (), max(1, total - limit), min(limit, total - 1) + 1)
        return jnp.stack([one, total - one])
    sizes = jnp.asarray(length_profile(count, total, limit, slope), jnp.int32)
    twos = (count - 1) // 2
    source_of, receiver = sizes[1:1 + 2 * twos:2], sizes[2:2 + 2 * twos:2]
    slack = jnp.minimum(source_of - 1, limit - receiver)
    moved = jax.random.randint(jax.random.fold_in(key, 1), (twos,), 0, 1 << 20) % (slack + 1)
    sizes = sizes.at[1:1 + 2 * twos:2].set(source_of - moved).at[2:2 + 2 * twos:2].set(receiver + moved)
    return sizes[jax.random.permutation(jax.random.fold_in(key, 2), count)]


def centred(own_key, dims, spread, limit, pieces=(), held_as=jnp.bfloat16):
    level = block_levels(own_key, dims, pieces, -0.22, 0.18) if pieces else 1.0
    drawn = jax.random.normal(own_key, dims, jnp.float32) * spread * level
    return jnp.minimum(jnp.maximum(drawn, -limit), limit).astype(held_as)


def setup_inputs(seed: int = 0) -> dict:
    keys = jax.random.split(jax.random.key(seed), 13)
    layer_input = centred(keys[0], (TOKENS, D), 1.0, 6.0, ((0, 128),))
    queries = draw_queries(jax.random.fold_in(keys[12], 71), 0)
    suffix_kv = centred(keys[2], (TOKENS, KVW), 1.0, 6.0, ((0, 128),))
    past_kv = centred(keys[3], (REQS * PAST_DEV, KVW), 1.0, 6.0, ((0, 128),))
    prefix_kv = centred(keys[4], (N_GROUP * PREFIX, KVW), 1.0, 6.0, ((0, 128),))
    suffix_len = uneven(keys[5], REQS, 3 * TOK_DEV * REQS // 4, TOK_DEV, 2).astype(jnp.int32)
    past_len = uneven(keys[6], REQS, PAST_DEV * REQS // 2, PAST_DEV, 2).astype(jnp.int32)
    out_weight = centred(keys[7], (QW, D), QW ** -0.5, 0.109375, ((0, 8),))
    norm_gain = jnp.clip(1.0 + 0.1 * jax.random.normal(keys[8], (D,), jnp.float32), 0.5, 1.5).astype(jnp.bfloat16)
    gate_weight = centred(keys[9], (D, FF), D ** -0.5, 0.109375, ((1, 16),))
    up_weight = centred(keys[10], (D, FF), D ** -0.5, 0.109375, ((1, 16),))
    down_weight = centred(keys[11], (FF, D), FF ** -0.5, 0.0625, ((0, 16),))
    return dict(layer_input=layer_input, queries=queries, suffix_kv=suffix_kv, past_kv=past_kv, prefix_kv=prefix_kv, suffix_len=suffix_len, past_len=past_len, out_weight=out_weight, norm_gain=norm_gain, gate_weight=gate_weight, up_weight=up_weight, down_weight=down_weight)


def attend(query_rows, key_rows, key_pos, key_valid, query_pos):
    count = query_rows.shape[0]
    total_keys = key_rows.shape[0]
    ratio = HEADS // KV_HEADS
    query_heads = query_rows.astype(jnp.float32).reshape(count, KV_HEADS, ratio, HEAD)
    key_heads = key_rows[:, :KV_HEADS * HEAD].astype(jnp.float32).reshape(total_keys, KV_HEADS, HEAD)
    value_heads = key_rows[:, KV_HEADS * HEAD:].astype(jnp.float32).reshape(total_keys, KV_HEADS, HEAD)
    scores = jnp.einsum('skgh,nkh->kgsn', query_heads, key_heads) * HEAD ** (-0.5)
    near = query_pos[:, None] - key_pos[None, :] < WINDOW
    allowed = key_valid[None, :] & (key_pos[None, :] <= query_pos[:, None]) & ((key_pos[None, :] < SINK) | near)
    scores = jnp.where(allowed, scores, -1e+30)
    largest = lax.optimization_barrier(jnp.max(scores, axis=-1, keepdims=True))
    expo = jnp.where(allowed, jnp.exp(scores - largest), 0.0)
    denom = lax.optimization_barrier(jnp.sum(expo, axis=-1))
    probs = lax.optimization_barrier(expo.astype(jnp.bfloat16)).astype(jnp.float32)
    summed = jnp.einsum('kgsn,nkh->kgsh', probs, value_heads)
    result = summed / denom[..., None]
    return result.transpose(2, 0, 1, 3).reshape(count, HEADS * HEAD).astype(jnp.bfloat16)

def reference(layer_input, queries, suffix_kv, past_kv, prefix_kv, suffix_len, past_len, out_weight, norm_gain, gate_weight, up_weight, down_weight):

    def one_request(index):
        group_index = index // N_REQ
        query_rows = lax.dynamic_slice_in_dim(queries, index * TOK_DEV, TOK_DEV, 0)
        own_rows = lax.dynamic_slice_in_dim(suffix_kv, index * TOK_DEV, TOK_DEV, 0)
        past_rows = lax.dynamic_slice_in_dim(past_kv, index * PAST_DEV, PAST_DEV, 0)
        prefix_rows = lax.dynamic_slice_in_dim(prefix_kv, group_index * PREFIX, PREFIX, 0)
        past_count = past_len[index]
        offsets = jnp.arange(TOK_DEV, dtype=jnp.int32)
        query_pos = PREFIX + past_count + offsets
        key_rows = jnp.concatenate([prefix_rows, past_rows, own_rows], axis=0)
        key_pos = jnp.concatenate([jnp.arange(PREFIX, dtype=jnp.int32), PREFIX + jnp.arange(PAST_DEV, dtype=jnp.int32), query_pos])
        key_valid = jnp.concatenate([jnp.ones((PREFIX,), bool), jnp.arange(PAST_DEV, dtype=jnp.int32) < past_count, jnp.ones((TOK_DEV,), bool)])
        return attend(query_rows, key_rows, key_pos, key_valid, query_pos)
    attended = lax.map(one_request, jnp.arange(REQS, dtype=jnp.int32)).reshape(TOKENS, HEADS * HEAD)
    mixed = layer_input.astype(jnp.float32) + jnp.dot(attended, out_weight, preferred_element_type=jnp.float32)
    scale = lax.rsqrt(lax.optimization_barrier(jnp.mean(mixed * mixed, axis=-1, keepdims=True)) + 1e-05)
    normed = (mixed * scale * norm_gain.astype(jnp.float32)).astype(jnp.bfloat16)
    down_blocks = down_weight.astype(jnp.float32).reshape(N_REQ, FF // N_REQ, D)

    def feed_block(rows):
        gate = jnp.dot(rows, gate_weight, preferred_element_type=jnp.float32)
        upper = jnp.dot(rows, up_weight, preferred_element_type=jnp.float32)
        hidden = (jax.nn.silu(gate) * upper).astype(jnp.bfloat16)
        shards = hidden.reshape(rows.shape[0], N_REQ, FF // N_REQ).astype(jnp.float32)
        parts = jnp.einsum('tkf,kfd->ktd', shards, down_blocks)
        parts = lax.optimization_barrier(parts.astype(jnp.bfloat16)).astype(jnp.float32)
        return lax.optimization_barrier(jnp.sum(parts, axis=0))
    feed = lax.map(feed_block, normed.reshape(REQS, TOK_DEV, D)).reshape(TOKENS, D)
    live = (jnp.arange(TOK_DEV, dtype=jnp.int32)[None, :] < suffix_len[:, None]).reshape(TOKENS)
    return jnp.where(live[:, None], mixed + feed, 0.0).astype(jnp.bfloat16)
```

```python
import jax
import jax.numpy as jnp
from jax import lax
from jax.sharding import PartitionSpec as P

HEADS = 24
KV_HEADS = 8
HEAD = 128
SINK = 4


def absorb(state, query_heads, key_rows, key_pos, key_valid, query_pos, window):
    maxima, totals, sums = state
    count = key_rows.shape[0]
    key_heads = key_rows[:, : KV_HEADS * HEAD].reshape(count, KV_HEADS, HEAD)
    value_heads = key_rows[:, KV_HEADS * HEAD :].reshape(count, KV_HEADS, HEAD)
    scores = jnp.einsum(
        "skgh,nkh->kgsn", query_heads, key_heads, preferred_element_type=jnp.float32
    ) * HEAD ** (-0.5)
    near = query_pos[:, None] - key_pos[None, :] < window
    allowed = (
        key_valid[None, :]
        & (key_pos[None, :] <= query_pos[:, None])
        & ((key_pos[None, :] < SINK) | near)
    )
    scores = jnp.where(allowed, scores, -1e30)
    new_max = jnp.maximum(maxima, jnp.max(scores, axis=-1))
    expo = jnp.where(allowed, jnp.exp(scores - new_max[..., None]), 0.0)
    factor = jnp.exp(maxima - new_max)
    totals = totals * factor + jnp.sum(expo, axis=-1)
    sums = sums * factor[..., None] + jnp.einsum(
        "kgsn,nkh->kgsh", expo.astype(jnp.bfloat16), value_heads, preferred_element_type=jnp.float32
    )
    return (new_max, totals, sums)


def shards(
    layer_input,
    queries,
    suffix_kv,
    past_kv,
    prefix_kv,
    suffix_len,
    past_len,
    out_weight,
    norm_gain,
    gate_weight,
    up_weight,
    down_weight,
):
    rows_here = queries.shape[0]
    past_slots = past_kv.shape[0]
    prefix_total = prefix_kv.shape[0] * lax.axis_size("req")
    window = prefix_total + past_slots // 2
    past_count = past_len[0]
    offsets = jnp.arange(rows_here, dtype=jnp.int32)
    query_pos = prefix_total + past_count + offsets
    ratio = HEADS // KV_HEADS
    query_heads = queries.reshape(rows_here, KV_HEADS, ratio, HEAD)
    state = (
        jnp.full((KV_HEADS, ratio, rows_here), -1e30, jnp.float32),
        jnp.zeros((KV_HEADS, ratio, rows_here), jnp.float32),
        jnp.zeros((KV_HEADS, ratio, rows_here, HEAD), jnp.float32),
    )
    local_rows = jnp.concatenate([past_kv, suffix_kv], axis=0)
    local_pos = jnp.concatenate([prefix_total + jnp.arange(past_slots, dtype=jnp.int32), query_pos])
    local_valid = jnp.concatenate(
        [jnp.arange(past_slots, dtype=jnp.int32) < past_count, jnp.ones((rows_here,), bool)]
    )
    state = absorb(state, query_heads, local_rows, local_pos, local_valid, query_pos, window)
    n_req = lax.axis_size("req")
    piece = lax.all_to_all(
        jnp.broadcast_to(prefix_kv[None], (n_req,) + prefix_kv.shape), "req", 0, 0, tiled=False
    ).reshape(prefix_total, prefix_kv.shape[1])
    count = piece.shape[0]
    positions = jnp.arange(count, dtype=jnp.int32)
    maxima, totals, sums = absorb(
        state, query_heads, piece, positions, jnp.ones((count,), bool), query_pos, window
    )
    attended = (
        (sums / totals[..., None])
        .transpose(2, 0, 1, 3)
        .reshape(rows_here, HEADS * HEAD)
        .astype(jnp.bfloat16)
    )
    n_group = lax.axis_size("group")
    block = out_weight.shape[0]
    columns = lax.all_to_all(
        attended.reshape(rows_here, n_group, block), "group", 1, 0, tiled=False
    ).reshape(n_group * rows_here, block)
    partial = jnp.dot(columns, out_weight, preferred_element_type=jnp.float32).astype(jnp.bfloat16)
    returned = lax.all_to_all(
        partial.reshape(n_group, rows_here, partial.shape[1]), "group", 0, 0, tiled=False
    )
    projected = jnp.sum(returned.astype(jnp.float32), axis=0)
    mixed = layer_input.astype(jnp.float32) + projected
    scale = lax.rsqrt(jnp.mean(mixed * mixed, axis=-1, keepdims=True) + 1e-05)
    normed = (mixed * scale * norm_gain.astype(jnp.float32)).astype(jnp.bfloat16)
    gathered = lax.all_gather(normed, "req", axis=0, tiled=True)
    gate = jnp.dot(gathered, gate_weight, preferred_element_type=jnp.float32)
    upper = jnp.dot(gathered, up_weight, preferred_element_type=jnp.float32)
    hidden = (jax.nn.silu(gate) * upper).astype(jnp.bfloat16)
    feed = lax.psum_scatter(
        jnp.dot(hidden, down_weight, preferred_element_type=jnp.float32).astype(jnp.bfloat16),
        "req",
        scatter_dimension=0,
        tiled=True,
    ).astype(jnp.float32)
    live = offsets < suffix_len[0]
    return jnp.where(live[:, None], mixed + feed, 0.0).astype(jnp.bfloat16)


def solution(mesh):
    in_specs = (
        P(("group", "req"), None),
        P(("group", "req"), None),
        P(("group", "req"), None),
        P(("group", "req"), None),
        P(("group", "req"), None),
        P(("group", "req")),
        P(("group", "req")),
        P("group", None),
        P(),
        P(None, "req"),
        P(None, "req"),
        P("req", None),
    )
    out_specs = P(("group", "req"), None)
    return jax.shard_map(shards, mesh=mesh, in_specs=in_specs, out_specs=out_specs, check_vma=False)
```

```python
import jax
import jax.numpy as jnp
from jax import lax
from jax.sharding import PartitionSpec as P

HEADS = 24
KV_HEADS = 8
HEAD = 128
SINK = 4


def absorb(state, query_heads, key_rows, key_pos, key_valid, query_pos, window):
    maxima, totals, sums = state
    count = key_rows.shape[0]
    key_heads = key_rows[:, : KV_HEADS * HEAD].reshape(count, KV_HEADS, HEAD)
    value_heads = key_rows[:, KV_HEADS * HEAD :].reshape(count, KV_HEADS, HEAD)
    scores = jnp.einsum(
        "skgh,nkh->kgsn", query_heads, key_heads, preferred_element_type=jnp.float32
    ) * HEAD ** (-0.5)
    near = query_pos[:, None] - key_pos[None, :] < window
    allowed = (
        key_valid[None, :]
        & (key_pos[None, :] <= query_pos[:, None])
        & ((key_pos[None, :] < SINK) | near)
    )
    scores = jnp.where(allowed, scores, -1e30)
    new_max = jnp.maximum(maxima, jnp.max(scores, axis=-1))
    expo = jnp.where(allowed, jnp.exp(scores - new_max[..., None]), 0.0)
    factor = jnp.exp(maxima - new_max)
    totals = totals * factor + jnp.sum(expo, axis=-1)
    sums = sums * factor[..., None] + jnp.einsum(
        "kgsn,nkh->kgsh", expo.astype(jnp.bfloat16), value_heads, preferred_element_type=jnp.float32
    )
    return (new_max, totals, sums)


def shards(
    layer_input,
    queries,
    suffix_kv,
    past_kv,
    prefix_kv,
    suffix_len,
    past_len,
    out_weight,
    norm_gain,
    gate_weight,
    up_weight,
    down_weight,
):
    rows_here = queries.shape[0]
    past_slots = past_kv.shape[0]
    prefix_total = prefix_kv.shape[0] * lax.axis_size("req")
    window = prefix_total + past_slots // 2
    past_count = past_len[0]
    offsets = jnp.arange(rows_here, dtype=jnp.int32)
    query_pos = prefix_total + past_count + offsets
    ratio = HEADS // KV_HEADS
    query_heads = queries.reshape(rows_here, KV_HEADS, ratio, HEAD)
    state = (
        jnp.full((KV_HEADS, ratio, rows_here), -1e30, jnp.float32),
        jnp.zeros((KV_HEADS, ratio, rows_here), jnp.float32),
        jnp.zeros((KV_HEADS, ratio, rows_here, HEAD), jnp.float32),
    )
    local_rows = jnp.concatenate([past_kv, suffix_kv], axis=0)
    local_pos = jnp.concatenate([prefix_total + jnp.arange(past_slots, dtype=jnp.int32), query_pos])
    local_valid = jnp.concatenate(
        [jnp.arange(past_slots, dtype=jnp.int32) < past_count, jnp.ones((rows_here,), bool)]
    )
    state = absorb(state, query_heads, local_rows, local_pos, local_valid, query_pos, window)
    n_req = lax.axis_size("req")
    piece = lax.all_to_all(
        jnp.broadcast_to(prefix_kv[None], (n_req,) + prefix_kv.shape), "req", 0, 0, tiled=False
    ).reshape(prefix_total, prefix_kv.shape[1])
    count = piece.shape[0]
    positions = jnp.arange(count, dtype=jnp.int32)
    maxima, totals, sums = absorb(
        state, query_heads, piece, positions, jnp.ones((count,), bool), query_pos, window
    )
    attended = (
        (sums / totals[..., None])
        .transpose(2, 0, 1, 3)
        .reshape(rows_here, HEADS * HEAD)
        .astype(jnp.bfloat16)
    )
    n_group = lax.axis_size("group")
    block = out_weight.shape[0]
    chunks = 2
    size = rows_here // chunks
    outputs = []
    for c in range(chunks):
        rows = slice(c * size, (c + 1) * size)
        columns = lax.all_to_all(
            attended[rows].reshape(size, n_group, block), "group", 1, 0, tiled=False
        ).reshape(n_group * size, block)
        partial = jnp.dot(columns, out_weight, preferred_element_type=jnp.float32).astype(
            jnp.bfloat16
        )
        returned = lax.all_to_all(
            partial.reshape(n_group, size, partial.shape[1]), "group", 0, 0, tiled=False
        )
        projected = jnp.sum(returned.astype(jnp.float32), axis=0)
        mixed = layer_input[rows].astype(jnp.float32) + projected
        scale = lax.rsqrt(jnp.mean(mixed * mixed, axis=-1, keepdims=True) + 1e-05)
        normed = (mixed * scale * norm_gain.astype(jnp.float32)).astype(jnp.bfloat16)
        gathered = lax.all_gather(normed, "req", axis=0, tiled=True)
        gate = jnp.dot(gathered, gate_weight, preferred_element_type=jnp.float32)
        upper = jnp.dot(gathered, up_weight, preferred_element_type=jnp.float32)
        hidden = (jax.nn.silu(gate) * upper).astype(jnp.bfloat16)
        feed = lax.psum_scatter(
            jnp.dot(hidden, down_weight, preferred_element_type=jnp.float32).astype(jnp.bfloat16),
            "req",
            scatter_dimension=0,
            tiled=True,
        ).astype(jnp.float32)
        live = offsets[rows] < suffix_len[0]
        outputs.append(jnp.where(live[:, None], mixed + feed, 0.0).astype(jnp.bfloat16))
    return jnp.concatenate(outputs, axis=0)


def solution(mesh):
    in_specs = (
        P(("group", "req"), None),
        P(("group", "req"), None),
        P(("group", "req"), None),
        P(("group", "req"), None),
        P(("group", "req"), None),
        P(("group", "req")),
        P(("group", "req")),
        P("group", None),
        P(),
        P(None, "req"),
        P(None, "req"),
        P("req", None),
    )
    out_specs = P(("group", "req"), None)
    return jax.shard_map(shards, mesh=mesh, in_specs=in_specs, out_specs=out_specs, check_vma=False)
```

```python
import jax
import jax.numpy as jnp
from jax import lax
from jax.sharding import PartitionSpec as P

HEADS = 24
KV_HEADS = 8
HEAD = 128
SINK = 4
GROUP = ("z", "x_lo")
REQ = ("x_hi", "y", "core")
ALL = GROUP + REQ


def absorb(state, query_heads, key_rows, key_pos, key_valid, query_pos, window):
    maxima, totals, sums = state
    count = key_rows.shape[0]
    key_heads = key_rows[:, : KV_HEADS * HEAD].reshape(count, KV_HEADS, HEAD)
    value_heads = key_rows[:, KV_HEADS * HEAD :].reshape(count, KV_HEADS, HEAD)
    scores = jnp.einsum(
        "skgh,nkh->kgsn", query_heads, key_heads, preferred_element_type=jnp.float32
    ) * HEAD ** (-0.5)
    near = query_pos[:, None] - key_pos[None, :] < window
    allowed = (
        key_valid[None, :]
        & (key_pos[None, :] <= query_pos[:, None])
        & ((key_pos[None, :] < SINK) | near)
    )
    scores = jnp.where(allowed, scores, -1e30)
    new_max = jnp.maximum(maxima, jnp.max(scores, axis=-1))
    expo = jnp.where(allowed, jnp.exp(scores - new_max[..., None]), 0.0)
    factor = jnp.exp(maxima - new_max)
    totals = totals * factor + jnp.sum(expo, axis=-1)
    sums = sums * factor[..., None] + jnp.einsum(
        "kgsn,nkh->kgsh", expo.astype(jnp.bfloat16), value_heads, preferred_element_type=jnp.float32
    )
    return (new_max, totals, sums)


def shards(
    layer_input,
    queries,
    suffix_kv,
    past_kv,
    prefix_kv,
    suffix_len,
    past_len,
    out_weight,
    norm_gain,
    gate_weight,
    up_weight,
    down_weight,
):
    rows_here = queries.shape[0]
    past_slots = past_kv.shape[0]
    prefix_total = prefix_kv.shape[0] * lax.axis_size(REQ)
    window = prefix_total + past_slots // 2
    past_count = past_len[0]
    offsets = jnp.arange(rows_here, dtype=jnp.int32)
    query_pos = prefix_total + past_count + offsets
    ratio = HEADS // KV_HEADS
    query_heads = queries.reshape(rows_here, KV_HEADS, ratio, HEAD)
    state = (
        jnp.full((KV_HEADS, ratio, rows_here), -1e30, jnp.float32),
        jnp.zeros((KV_HEADS, ratio, rows_here), jnp.float32),
        jnp.zeros((KV_HEADS, ratio, rows_here, HEAD), jnp.float32),
    )
    local_rows = jnp.concatenate([past_kv, suffix_kv], axis=0)
    local_pos = jnp.concatenate([prefix_total + jnp.arange(past_slots, dtype=jnp.int32), query_pos])
    local_valid = jnp.concatenate(
        [jnp.arange(past_slots, dtype=jnp.int32) < past_count, jnp.ones((rows_here,), bool)]
    )
    state = absorb(state, query_heads, local_rows, local_pos, local_valid, query_pos, window)
    n_req = lax.axis_size(REQ)
    piece = lax.all_to_all(
        jnp.broadcast_to(prefix_kv[None], (n_req,) + prefix_kv.shape), REQ, 0, 0, tiled=False
    ).reshape(prefix_total, prefix_kv.shape[1])
    count = piece.shape[0]
    positions = jnp.arange(count, dtype=jnp.int32)
    maxima, totals, sums = absorb(
        state, query_heads, piece, positions, jnp.ones((count,), bool), query_pos, window
    )
    attended = (
        (sums / totals[..., None])
        .transpose(2, 0, 1, 3)
        .reshape(rows_here, HEADS * HEAD)
        .astype(jnp.bfloat16)
    )
    pair = lax.all_gather(out_weight, "x_lo", axis=0, tiled=True)
    n_z = lax.axis_size("z")
    block = pair.shape[0]
    columns = lax.all_to_all(
        attended.reshape(rows_here, n_z, block), "z", 1, 0, tiled=False
    ).reshape(n_z * rows_here, block)
    partial = jnp.dot(columns, pair, preferred_element_type=jnp.float32).astype(jnp.bfloat16)
    returned = lax.all_to_all(
        partial.reshape(n_z, rows_here, partial.shape[1]), "z", 0, 0, tiled=False
    )
    projected = jnp.sum(returned.astype(jnp.float32), axis=0)
    mixed = layer_input.astype(jnp.float32) + projected
    scale = lax.rsqrt(jnp.mean(mixed * mixed, axis=-1, keepdims=True) + 1e-05)
    normed = (mixed * scale * norm_gain.astype(jnp.float32)).astype(jnp.bfloat16)
    swap = [(0, 1), (1, 0)]
    gate_both = jnp.concatenate([gate_weight, lax.ppermute(gate_weight, "core", swap)], axis=1)
    up_both = jnp.concatenate([up_weight, lax.ppermute(up_weight, "core", swap)], axis=1)
    down_both = jnp.concatenate([down_weight, lax.ppermute(down_weight, "core", swap)], axis=0)
    gathered = lax.all_gather(normed, ("x_hi", "y"), axis=0, tiled=True)
    gate = jnp.dot(gathered, gate_both, preferred_element_type=jnp.float32)
    upper = jnp.dot(gathered, up_both, preferred_element_type=jnp.float32)
    hidden = (jax.nn.silu(gate) * upper).astype(jnp.bfloat16)
    feed = lax.psum_scatter(
        jnp.dot(hidden, down_both, preferred_element_type=jnp.float32).astype(jnp.bfloat16),
        ("x_hi", "y"),
        scatter_dimension=0,
        tiled=True,
    ).astype(jnp.float32)
    live = offsets < suffix_len[0]
    return jnp.where(live[:, None], mixed + feed, 0.0).astype(jnp.bfloat16)


def solution(mesh):
    sizes = [mesh.shape["group"] // 2, 2, 2, mesh.shape["req"] // 4, 2]
    fine = jax.sharding.Mesh(mesh.devices.reshape(sizes), ALL)
    in_specs = (
        P(ALL, None),
        P(ALL, None),
        P(ALL, None),
        P(ALL, None),
        P(ALL, None),
        P(ALL),
        P(ALL),
        P(GROUP, None),
        P(),
        P(None, REQ),
        P(None, REQ),
        P(REQ, None),
    )
    out_specs = P(ALL, None)
    return jax.shard_map(shards, mesh=fine, in_specs=in_specs, out_specs=out_specs, check_vma=False)
```

```python
import jax
import jax.numpy as jnp
from jax import lax
from jax.sharding import PartitionSpec as P

HEADS = 24
KV_HEADS = 8
HEAD = 128
SINK = 4
GROUP = ("z", "x_lo")
REQ = ("x_hi", "y", "core")
ALL = GROUP + REQ


def absorb(state, query_heads, key_rows, key_pos, key_valid, query_pos, window):
    maxima, totals, sums = state
    count = key_rows.shape[0]
    key_heads = key_rows[:, : KV_HEADS * HEAD].reshape(count, KV_HEADS, HEAD)
    value_heads = key_rows[:, KV_HEADS * HEAD :].reshape(count, KV_HEADS, HEAD)
    scores = jnp.einsum(
        "skgh,nkh->kgsn", query_heads, key_heads, preferred_element_type=jnp.float32
    ) * HEAD ** (-0.5)
    near = query_pos[:, None] - key_pos[None, :] < window
    allowed = (
        key_valid[None, :]
        & (key_pos[None, :] <= query_pos[:, None])
        & ((key_pos[None, :] < SINK) | near)
    )
    scores = jnp.where(allowed, scores, -1e30)
    new_max = jnp.maximum(maxima, jnp.max(scores, axis=-1))
    expo = jnp.where(allowed, jnp.exp(scores - new_max[..., None]), 0.0)
    factor = jnp.exp(maxima - new_max)
    totals = totals * factor + jnp.sum(expo, axis=-1)
    sums = sums * factor[..., None] + jnp.einsum(
        "kgsn,nkh->kgsh", expo.astype(jnp.bfloat16), value_heads, preferred_element_type=jnp.float32
    )
    return (new_max, totals, sums)


def shards(
    layer_input,
    queries,
    suffix_kv,
    past_kv,
    prefix_kv,
    suffix_len,
    past_len,
    out_weight,
    norm_gain,
    gate_weight,
    up_weight,
    down_weight,
):
    rows_here = queries.shape[0]
    past_slots = past_kv.shape[0]
    prefix_total = prefix_kv.shape[0] * lax.axis_size(REQ)
    window = prefix_total + past_slots // 2
    past_count = past_len[0]
    offsets = jnp.arange(rows_here, dtype=jnp.int32)
    query_pos = prefix_total + past_count + offsets
    ratio = HEADS // KV_HEADS
    query_heads = queries.reshape(rows_here, KV_HEADS, ratio, HEAD)
    state = (
        jnp.full((KV_HEADS, ratio, rows_here), -1e30, jnp.float32),
        jnp.zeros((KV_HEADS, ratio, rows_here), jnp.float32),
        jnp.zeros((KV_HEADS, ratio, rows_here, HEAD), jnp.float32),
    )
    local_rows = jnp.concatenate([past_kv, suffix_kv], axis=0)
    local_pos = jnp.concatenate([prefix_total + jnp.arange(past_slots, dtype=jnp.int32), query_pos])
    local_valid = jnp.concatenate(
        [jnp.arange(past_slots, dtype=jnp.int32) < past_count, jnp.ones((rows_here,), bool)]
    )
    state = absorb(state, query_heads, local_rows, local_pos, local_valid, query_pos, window)
    n_req = lax.axis_size(REQ)
    piece = lax.all_to_all(
        jnp.broadcast_to(prefix_kv[None], (n_req,) + prefix_kv.shape), REQ, 0, 0, tiled=False
    ).reshape(prefix_total, prefix_kv.shape[1])
    count = piece.shape[0]
    positions = jnp.arange(count, dtype=jnp.int32)
    maxima, totals, sums = absorb(
        state, query_heads, piece, positions, jnp.ones((count,), bool), query_pos, window
    )
    attended = (
        (sums / totals[..., None])
        .transpose(2, 0, 1, 3)
        .reshape(rows_here, HEADS * HEAD)
        .astype(jnp.bfloat16)
    )
    pair = jnp.concatenate([out_weight, lax.ppermute(out_weight, "x_lo", [(0, 1), (1, 0)])])
    n_z = lax.axis_size("z")
    block = pair.shape[0]
    halves = attended.reshape(rows_here, n_z, 2, out_weight.shape[0])
    halves = jnp.where(lax.axis_index("x_lo") == 0, halves, halves[:, :, ::-1])
    columns = lax.all_to_all(
        halves.reshape(rows_here, n_z, block), "z", 1, 0, tiled=False
    ).reshape(n_z * rows_here, block)
    partial = jnp.dot(columns, pair, preferred_element_type=jnp.float32).astype(jnp.bfloat16)
    returned = lax.all_to_all(
        partial.reshape(n_z, rows_here, partial.shape[1]), "z", 0, 0, tiled=False
    )
    projected = jnp.sum(returned.astype(jnp.float32), axis=0)
    mixed = layer_input.astype(jnp.float32) + projected
    scale = lax.rsqrt(jnp.mean(mixed * mixed, axis=-1, keepdims=True) + 1e-05)
    normed = (mixed * scale * norm_gain.astype(jnp.float32)).astype(jnp.bfloat16)
    swap = [(0, 1), (1, 0)]
    gate_both = jnp.concatenate([gate_weight, lax.ppermute(gate_weight, "core", swap)], axis=1)
    up_both = jnp.concatenate([up_weight, lax.ppermute(up_weight, "core", swap)], axis=1)
    down_both = jnp.concatenate([down_weight, lax.ppermute(down_weight, "core", swap)], axis=0)
    gathered = lax.all_gather(normed, ("x_hi", "y"), axis=0, tiled=True)
    gate = jnp.dot(gathered, gate_both, preferred_element_type=jnp.float32)
    upper = jnp.dot(gathered, up_both, preferred_element_type=jnp.float32)
    hidden = (jax.nn.silu(gate) * upper).astype(jnp.bfloat16)
    feed = lax.psum_scatter(
        jnp.dot(hidden, down_both, preferred_element_type=jnp.float32).astype(jnp.bfloat16),
        ("x_hi", "y"),
        scatter_dimension=0,
        tiled=True,
    ).astype(jnp.float32)
    live = offsets < suffix_len[0]
    return jnp.where(live[:, None], mixed + feed, 0.0).astype(jnp.bfloat16)


def solution(mesh):
    sizes = [mesh.shape["group"] // 2, 2, 2, mesh.shape["req"] // 4, 2]
    fine = jax.sharding.Mesh(mesh.devices.reshape(sizes), ALL)
    in_specs = (
        P(ALL, None),
        P(ALL, None),
        P(ALL, None),
        P(ALL, None),
        P(ALL, None),
        P(ALL),
        P(ALL),
        P(GROUP, None),
        P(),
        P(None, REQ),
        P(None, REQ),
        P(REQ, None),
    )
    out_specs = P(ALL, None)
    return jax.shard_map(shards, mesh=fine, in_specs=in_specs, out_specs=out_specs, check_vma=False)
```

```python
import jax
import jax.numpy as jnp
from jax import lax
from jax.sharding import PartitionSpec as P

HEADS = 24
KV_HEADS = 8
HEAD = 128
SINK = 4
GROUP = ("z", "x_lo")
REQ = ("x_hi", "y", "core")
ALL = GROUP + REQ


def absorb(state, query_heads, key_rows, key_pos, key_valid, query_pos, window):
    maxima, totals, sums = state
    count = key_rows.shape[0]
    key_heads = key_rows[:, : KV_HEADS * HEAD].reshape(count, KV_HEADS, HEAD)
    value_heads = key_rows[:, KV_HEADS * HEAD :].reshape(count, KV_HEADS, HEAD)
    scores = jnp.einsum(
        "skgh,nkh->kgsn", query_heads, key_heads, preferred_element_type=jnp.float32
    ) * HEAD ** (-0.5)
    near = query_pos[:, None] - key_pos[None, :] < window
    allowed = (
        key_valid[None, :]
        & (key_pos[None, :] <= query_pos[:, None])
        & ((key_pos[None, :] < SINK) | near)
    )
    scores = jnp.where(allowed, scores, -1e30)
    new_max = jnp.maximum(maxima, jnp.max(scores, axis=-1))
    expo = jnp.where(allowed, jnp.exp(scores - new_max[..., None]), 0.0)
    factor = jnp.exp(maxima - new_max)
    totals = totals * factor + jnp.sum(expo, axis=-1)
    sums = sums * factor[..., None] + jnp.einsum(
        "kgsn,nkh->kgsh", expo.astype(jnp.bfloat16), value_heads, preferred_element_type=jnp.float32
    )
    return (new_max, totals, sums)


def shards(
    layer_input,
    queries,
    suffix_kv,
    past_kv,
    prefix_kv,
    suffix_len,
    past_len,
    out_weight,
    norm_gain,
    gate_weight,
    up_weight,
    down_weight,
):
    rows_here = queries.shape[0]
    past_slots = past_kv.shape[0]
    prefix_total = prefix_kv.shape[0] * lax.axis_size(REQ)
    window = prefix_total + past_slots // 2
    past_count = past_len[0]
    offsets = jnp.arange(rows_here, dtype=jnp.int32)
    query_pos = prefix_total + past_count + offsets
    ratio = HEADS // KV_HEADS
    query_heads = queries.reshape(rows_here, KV_HEADS, ratio, HEAD)
    state = (
        jnp.full((KV_HEADS, ratio, rows_here), -1e30, jnp.float32),
        jnp.zeros((KV_HEADS, ratio, rows_here), jnp.float32),
        jnp.zeros((KV_HEADS, ratio, rows_here, HEAD), jnp.float32),
    )
    local_rows = jnp.concatenate([past_kv, suffix_kv], axis=0)
    local_pos = jnp.concatenate([prefix_total + jnp.arange(past_slots, dtype=jnp.int32), query_pos])
    local_valid = jnp.concatenate(
        [jnp.arange(past_slots, dtype=jnp.int32) < past_count, jnp.ones((rows_here,), bool)]
    )
    state = absorb(state, query_heads, local_rows, local_pos, local_valid, query_pos, window)
    n_req = lax.axis_size(REQ)
    piece = lax.all_to_all(
        jnp.broadcast_to(prefix_kv[None], (n_req,) + prefix_kv.shape), REQ, 0, 0, tiled=False
    ).reshape(prefix_total, prefix_kv.shape[1])
    count = piece.shape[0]
    positions = jnp.arange(count, dtype=jnp.int32)
    maxima, totals, sums = absorb(
        state, query_heads, piece, positions, jnp.ones((count,), bool), query_pos, window
    )
    attended = (
        (sums / totals[..., None])
        .transpose(2, 0, 1, 3)
        .reshape(rows_here, HEADS * HEAD)
        .astype(jnp.bfloat16)
    )
    pair = jnp.concatenate([out_weight, lax.ppermute(out_weight, "x_lo", [(0, 1), (1, 0)])])
    n_z = lax.axis_size("z")
    block = pair.shape[0]
    halves = attended.reshape(rows_here, n_z, 2, out_weight.shape[0])
    halves = jnp.where(lax.axis_index("x_lo") == 0, halves, halves[:, :, ::-1])
    columns = lax.all_to_all(
        halves.reshape(rows_here, n_z, block), "z", 1, 0, tiled=False
    ).reshape(n_z * rows_here, block)
    partial = jnp.dot(columns, pair, preferred_element_type=jnp.float32).astype(jnp.bfloat16)
    returned = lax.all_to_all(
        partial.reshape(n_z, rows_here, partial.shape[1]), "z", 0, 0, tiled=False
    )
    projected = jnp.sum(returned.astype(jnp.float32), axis=0)
    mixed = layer_input.astype(jnp.float32) + projected
    scale = lax.rsqrt(jnp.mean(mixed * mixed, axis=-1, keepdims=True) + 1e-05)
    normed = (mixed * scale * norm_gain.astype(jnp.float32)).astype(jnp.bfloat16)
    swap = [(0, 1), (1, 0)]
    gate_both = jnp.concatenate([gate_weight, lax.ppermute(gate_weight, "core", swap)], axis=1)
    up_both = jnp.concatenate([up_weight, lax.ppermute(up_weight, "core", swap)], axis=1)
    down_both = jnp.concatenate([down_weight, lax.ppermute(down_weight, "core", swap)], axis=0)
    gathered = lax.all_gather(normed, ("x_hi", "y"), axis=0, tiled=True)
    gate = jnp.dot(gathered, gate_both, preferred_element_type=jnp.float32)
    upper = jnp.dot(gathered, up_both, preferred_element_type=jnp.float32)
    hidden = (jax.nn.silu(gate) * upper).astype(jnp.bfloat16)
    parts = jnp.dot(hidden, down_both, preferred_element_type=jnp.float32).astype(jnp.bfloat16)
    parts = lax.all_to_all(
        parts.reshape(-1, rows_here, parts.shape[1]), ("x_hi", "y"), 0, 0, tiled=False
    )
    feed = jnp.sum(parts.astype(jnp.float32), axis=0)
    live = offsets < suffix_len[0]
    return jnp.where(live[:, None], mixed + feed, 0.0).astype(jnp.bfloat16)


def solution(mesh):
    sizes = [mesh.shape["group"] // 2, 2, 2, mesh.shape["req"] // 4, 2]
    fine = jax.sharding.Mesh(mesh.devices.reshape(sizes), ALL)
    in_specs = (
        P(ALL, None),
        P(ALL, None),
        P(ALL, None),
        P(ALL, None),
        P(ALL, None),
        P(ALL),
        P(ALL),
        P(GROUP, None),
        P(),
        P(None, REQ),
        P(None, REQ),
        P(REQ, None),
    )
    out_specs = P(ALL, None)
    return jax.shard_map(shards, mesh=fine, in_specs=in_specs, out_specs=out_specs, check_vma=False)
```

```python
import jax
import jax.numpy as jnp
from jax import lax
from jax.sharding import PartitionSpec as P

HEADS = 24
KV_HEADS = 8
HEAD = 128
SINK = 4
GROUP = ("z", "x_lo")
REQ = ("x_hi", "y", "core")
ALL = GROUP + REQ


def absorb(state, query_heads, key_rows, key_pos, key_valid, query_pos, window):
    maxima, totals, sums = state
    count = key_rows.shape[0]
    key_heads = key_rows[:, : KV_HEADS * HEAD].reshape(count, KV_HEADS, HEAD)
    value_heads = key_rows[:, KV_HEADS * HEAD :].reshape(count, KV_HEADS, HEAD)
    scores = jnp.einsum(
        "skgh,nkh->kgsn", query_heads, key_heads, preferred_element_type=jnp.float32
    ) * HEAD ** (-0.5)
    near = query_pos[:, None] - key_pos[None, :] < window
    allowed = (
        key_valid[None, :]
        & (key_pos[None, :] <= query_pos[:, None])
        & ((key_pos[None, :] < SINK) | near)
    )
    scores = jnp.where(allowed, scores, -1e30)
    new_max = jnp.maximum(maxima, jnp.max(scores, axis=-1))
    expo = jnp.where(allowed, jnp.exp(scores - new_max[..., None]), 0.0)
    factor = jnp.exp(maxima - new_max)
    totals = totals * factor + jnp.sum(expo, axis=-1)
    sums = sums * factor[..., None] + jnp.einsum(
        "kgsn,nkh->kgsh", expo.astype(jnp.bfloat16), value_heads, preferred_element_type=jnp.float32
    )
    return (new_max, totals, sums)


def shards(
    layer_input,
    queries,
    suffix_kv,
    past_kv,
    prefix_kv,
    suffix_len,
    past_len,
    out_weight,
    norm_gain,
    gate_weight,
    up_weight,
    down_weight,
):
    rows_here = queries.shape[0]
    past_slots = past_kv.shape[0]
    prefix_total = prefix_kv.shape[0] * lax.axis_size(REQ)
    window = prefix_total + past_slots // 2
    past_count = past_len[0]
    offsets = jnp.arange(rows_here, dtype=jnp.int32)
    query_pos = prefix_total + past_count + offsets
    ratio = HEADS // KV_HEADS
    query_heads = queries.reshape(rows_here, KV_HEADS, ratio, HEAD)
    state = (
        jnp.full((KV_HEADS, ratio, rows_here), -1e30, jnp.float32),
        jnp.zeros((KV_HEADS, ratio, rows_here), jnp.float32),
        jnp.zeros((KV_HEADS, ratio, rows_here, HEAD), jnp.float32),
    )
    local_rows = jnp.concatenate([past_kv, suffix_kv], axis=0)
    local_pos = jnp.concatenate([prefix_total + jnp.arange(past_slots, dtype=jnp.int32), query_pos])
    local_valid = jnp.concatenate(
        [jnp.arange(past_slots, dtype=jnp.int32) < past_count, jnp.ones((rows_here,), bool)]
    )
    state = absorb(state, query_heads, local_rows, local_pos, local_valid, query_pos, window)
    n_req = lax.axis_size(REQ)
    piece = lax.all_to_all(
        jnp.broadcast_to(prefix_kv[None], (n_req,) + prefix_kv.shape), REQ, 0, 0, tiled=False
    ).reshape(prefix_total, prefix_kv.shape[1])
    count = piece.shape[0]
    positions = jnp.arange(count, dtype=jnp.int32)
    maxima, totals, sums = absorb(
        state, query_heads, piece, positions, jnp.ones((count,), bool), query_pos, window
    )
    attended = (
        (sums / totals[..., None])
        .transpose(2, 0, 1, 3)
        .reshape(rows_here, HEADS * HEAD)
        .astype(jnp.bfloat16)
    )
    pair = jnp.concatenate([out_weight, lax.ppermute(out_weight, "x_lo", [(0, 1), (1, 0)])])
    n_z = lax.axis_size("z")
    block = pair.shape[0]
    halves = attended.reshape(rows_here, n_z, 2, out_weight.shape[0])
    halves = jnp.where(lax.axis_index("x_lo") == 0, halves, halves[:, :, ::-1])
    columns = lax.all_to_all(
        halves.reshape(rows_here, n_z, block), "z", 1, 0, tiled=False
    ).reshape(n_z * rows_here, block)
    partial = jnp.dot(columns, pair, preferred_element_type=jnp.float32).astype(jnp.bfloat16)
    returned = lax.all_to_all(
        partial.reshape(n_z, rows_here, partial.shape[1]), "z", 0, 0, tiled=False
    )
    projected = jnp.sum(returned.astype(jnp.float32), axis=0)
    mixed = layer_input.astype(jnp.float32) + projected
    scale = lax.rsqrt(jnp.mean(mixed * mixed, axis=-1, keepdims=True) + 1e-05)
    normed = (mixed * scale * norm_gain.astype(jnp.float32)).astype(jnp.bfloat16)
    swap = [(0, 1), (1, 0)]
    gate_both = jnp.concatenate([gate_weight, lax.ppermute(gate_weight, "core", swap)], axis=1)
    up_both = jnp.concatenate([up_weight, lax.ppermute(up_weight, "core", swap)], axis=1)
    down_both = jnp.concatenate([down_weight, lax.ppermute(down_weight, "core", swap)], axis=0)
    feed_axes = ("x_hi", "y")
    n_feed = lax.axis_size(feed_axes)
    half = rows_here // 2
    gathered = jnp.concatenate(
        [
            lax.all_gather(normed[:half], feed_axes, axis=0, tiled=True),
            lax.all_to_all(
                jnp.broadcast_to(normed[half:][None], (n_feed, half, normed.shape[1])),
                feed_axes,
                0,
                0,
                tiled=False,
            ).reshape(n_feed * half, normed.shape[1]),
        ]
    )
    gate = jnp.dot(gathered, gate_both, preferred_element_type=jnp.float32)
    upper = jnp.dot(gathered, up_both, preferred_element_type=jnp.float32)
    hidden = (jax.nn.silu(gate) * upper).astype(jnp.bfloat16)
    parts = jnp.dot(hidden, down_both, preferred_element_type=jnp.float32).astype(jnp.bfloat16)
    parts = lax.all_to_all(
        parts.reshape(2, n_feed, half, parts.shape[1]), feed_axes, 1, 1, tiled=False
    )
    feed = jnp.sum(parts.astype(jnp.float32), axis=1).reshape(rows_here, parts.shape[-1])
    live = offsets < suffix_len[0]
    return jnp.where(live[:, None], mixed + feed, 0.0).astype(jnp.bfloat16)


def solution(mesh):
    sizes = [mesh.shape["group"] // 2, 2, 2, mesh.shape["req"] // 4, 2]
    fine = jax.sharding.Mesh(mesh.devices.reshape(sizes), ALL)
    in_specs = (
        P(ALL, None),
        P(ALL, None),
        P(ALL, None),
        P(ALL, None),
        P(ALL, None),
        P(ALL),
        P(ALL),
        P(GROUP, None),
        P(),
        P(None, REQ),
        P(None, REQ),
        P(REQ, None),
    )
    out_specs = P(ALL, None)
    return jax.shard_map(shards, mesh=fine, in_specs=in_specs, out_specs=out_specs, check_vma=False)
```

```python
import jax
import jax.numpy as jnp
from jax import lax
from jax.sharding import PartitionSpec as P

HEADS = 24
KV_HEADS = 8
HEAD = 128
SINK = 4
GROUP = ("z", "x_lo")
REQ = ("x_hi", "y", "core")
ALL = GROUP + REQ


def absorb(state, query_heads, key_rows, key_pos, key_valid, query_pos, window):
    maxima, totals, sums = state
    count = key_rows.shape[0]
    key_heads = key_rows[:, : KV_HEADS * HEAD].reshape(count, KV_HEADS, HEAD)
    value_heads = key_rows[:, KV_HEADS * HEAD :].reshape(count, KV_HEADS, HEAD)
    scores = jnp.einsum(
        "skgh,nkh->kgsn", query_heads, key_heads, preferred_element_type=jnp.float32
    ) * HEAD ** (-0.5)
    near = query_pos[:, None] - key_pos[None, :] < window
    allowed = (
        key_valid[None, :]
        & (key_pos[None, :] <= query_pos[:, None])
        & ((key_pos[None, :] < SINK) | near)
    )
    scores = jnp.where(allowed, scores, -1e30)
    new_max = jnp.maximum(maxima, jnp.max(scores, axis=-1))
    expo = jnp.where(allowed, jnp.exp(scores - new_max[..., None]), 0.0)
    factor = jnp.exp(maxima - new_max)
    totals = totals * factor + jnp.sum(expo, axis=-1)
    sums = sums * factor[..., None] + jnp.einsum(
        "kgsn,nkh->kgsh", expo.astype(jnp.bfloat16), value_heads, preferred_element_type=jnp.float32
    )
    return (new_max, totals, sums)


def shards(
    layer_input,
    queries,
    suffix_kv,
    past_kv,
    prefix_kv,
    suffix_len,
    past_len,
    out_weight,
    norm_gain,
    gate_weight,
    up_weight,
    down_weight,
):
    rows_here = queries.shape[0]
    past_slots = past_kv.shape[0]
    prefix_total = prefix_kv.shape[0] * lax.axis_size(REQ)
    window = prefix_total + past_slots // 2
    past_count = past_len[0]
    offsets = jnp.arange(rows_here, dtype=jnp.int32)
    query_pos = prefix_total + past_count + offsets
    ratio = HEADS // KV_HEADS
    query_heads = queries.reshape(rows_here, KV_HEADS, ratio, HEAD)
    state = (
        jnp.full((KV_HEADS, ratio, rows_here), -1e30, jnp.float32),
        jnp.zeros((KV_HEADS, ratio, rows_here), jnp.float32),
        jnp.zeros((KV_HEADS, ratio, rows_here, HEAD), jnp.float32),
    )
    local_rows = jnp.concatenate([past_kv, suffix_kv], axis=0)
    local_pos = jnp.concatenate([prefix_total + jnp.arange(past_slots, dtype=jnp.int32), query_pos])
    local_valid = jnp.concatenate(
        [jnp.arange(past_slots, dtype=jnp.int32) < past_count, jnp.ones((rows_here,), bool)]
    )
    state = absorb(state, query_heads, local_rows, local_pos, local_valid, query_pos, window)
    n_req = lax.axis_size(REQ)
    piece = lax.all_to_all(
        jnp.broadcast_to(prefix_kv[None], (n_req,) + prefix_kv.shape), REQ, 0, 0, tiled=False
    ).reshape(prefix_total, prefix_kv.shape[1])
    count = piece.shape[0]
    positions = jnp.arange(count, dtype=jnp.int32)
    maxima, totals, sums = absorb(
        state, query_heads, piece, positions, jnp.ones((count,), bool), query_pos, window
    )
    attended = (
        (sums / totals[..., None])
        .transpose(2, 0, 1, 3)
        .reshape(rows_here, HEADS * HEAD)
        .astype(jnp.bfloat16)
    )
    pair = jnp.concatenate([out_weight, lax.ppermute(out_weight, "x_lo", [(0, 1), (1, 0)])])
    n_z = lax.axis_size("z")
    block = pair.shape[0]
    halves = attended.reshape(rows_here, n_z, 2, out_weight.shape[0])
    halves = jnp.where(lax.axis_index("x_lo") == 0, halves, halves[:, :, ::-1])
    columns = lax.all_to_all(
        halves.reshape(rows_here, n_z, block), "z", 1, 0, tiled=False
    ).reshape(n_z * rows_here, block)
    partial = jnp.dot(columns, pair, preferred_element_type=jnp.float32).astype(jnp.bfloat16)
    returned = lax.all_to_all(
        partial.reshape(n_z, rows_here, partial.shape[1]), "z", 0, 0, tiled=False
    )
    projected = jnp.sum(returned.astype(jnp.float32), axis=0)
    mixed = layer_input.astype(jnp.float32) + projected
    scale = lax.rsqrt(jnp.mean(mixed * mixed, axis=-1, keepdims=True) + 1e-05)
    normed = (mixed * scale * norm_gain.astype(jnp.float32)).astype(jnp.bfloat16)
    swap = [(0, 1), (1, 0)]
    gate_both = jnp.concatenate([gate_weight, lax.ppermute(gate_weight, "core", swap)], axis=1)
    up_both = jnp.concatenate([up_weight, lax.ppermute(up_weight, "core", swap)], axis=1)
    down_both = jnp.concatenate([down_weight, lax.ppermute(down_weight, "core", swap)], axis=0)
    feed_axes = ("x_hi", "y")
    n_feed = lax.axis_size(feed_axes)
    gathered = lax.all_to_all(
        jnp.broadcast_to(normed[None], (n_feed,) + normed.shape), feed_axes, 0, 0, tiled=False
    ).reshape(n_feed * rows_here, normed.shape[1])
    gate = jnp.dot(gathered, gate_both, preferred_element_type=jnp.float32)
    upper = jnp.dot(gathered, up_both, preferred_element_type=jnp.float32)
    hidden = (jax.nn.silu(gate) * upper).astype(jnp.bfloat16)
    parts = jnp.dot(hidden, down_both, preferred_element_type=jnp.float32).astype(jnp.bfloat16)
    parts = lax.all_to_all(
        parts.reshape(n_feed, rows_here, parts.shape[1]), feed_axes, 0, 0, tiled=False
    )
    feed = jnp.sum(parts.astype(jnp.float32), axis=0)
    live = offsets < suffix_len[0]
    return jnp.where(live[:, None], mixed + feed, 0.0).astype(jnp.bfloat16)


def solution(mesh):
    sizes = [mesh.shape["group"] // 2, 2, 2, mesh.shape["req"] // 4, 2]
    fine = jax.sharding.Mesh(mesh.devices.reshape(sizes), ALL)
    in_specs = (
        P(ALL, None),
        P(ALL, None),
        P(ALL, None),
        P(ALL, None),
        P(ALL, None),
        P(ALL),
        P(ALL),
        P(GROUP, None),
        P(),
        P(None, REQ),
        P(None, REQ),
        P(REQ, None),
    )
    out_specs = P(ALL, None)
    return jax.shard_map(shards, mesh=fine, in_specs=in_specs, out_specs=out_specs, check_vma=False)
```

```python
import jax
import jax.numpy as jnp
from jax import lax
from jax.sharding import PartitionSpec as P

HEADS = 24
KV_HEADS = 8
HEAD = 128
SINK = 4
GROUP = ("z", "x_lo")
REQ = ("x_hi", "y", "core")
ALL = GROUP + REQ


def absorb(state, query_heads, key_rows, key_pos, key_valid, query_pos, window):
    maxima, totals, sums = state
    count = key_rows.shape[0]
    key_heads = key_rows[:, : KV_HEADS * HEAD].reshape(count, KV_HEADS, HEAD)
    value_heads = key_rows[:, KV_HEADS * HEAD :].reshape(count, KV_HEADS, HEAD)
    scores = jnp.einsum(
        "skgh,nkh->kgsn", query_heads, key_heads, preferred_element_type=jnp.float32
    ) * HEAD ** (-0.5)
    near = query_pos[:, None] - key_pos[None, :] < window
    allowed = (
        key_valid[None, :]
        & (key_pos[None, :] <= query_pos[:, None])
        & ((key_pos[None, :] < SINK) | near)
    )
    scores = jnp.where(allowed, scores, -1e30)
    new_max = jnp.maximum(maxima, jnp.max(scores, axis=-1))
    expo = jnp.where(allowed, jnp.exp(scores - new_max[..., None]), 0.0)
    factor = jnp.exp(maxima - new_max)
    totals = totals * factor + jnp.sum(expo, axis=-1)
    sums = sums * factor[..., None] + jnp.einsum(
        "kgsn,nkh->kgsh", expo.astype(jnp.bfloat16), value_heads, preferred_element_type=jnp.float32
    )
    return (new_max, totals, sums)


def shards(
    layer_input,
    queries,
    suffix_kv,
    past_kv,
    prefix_kv,
    suffix_len,
    past_len,
    out_weight,
    norm_gain,
    gate_weight,
    up_weight,
    down_weight,
):
    rows_here = queries.shape[0]
    past_slots = past_kv.shape[0]
    prefix_total = prefix_kv.shape[0] * lax.axis_size(REQ)
    window = prefix_total + past_slots // 2
    past_count = past_len[0]
    offsets = jnp.arange(rows_here, dtype=jnp.int32)
    query_pos = prefix_total + past_count + offsets
    ratio = HEADS // KV_HEADS
    query_heads = queries.reshape(rows_here, KV_HEADS, ratio, HEAD)
    state = (
        jnp.full((KV_HEADS, ratio, rows_here), -1e30, jnp.float32),
        jnp.zeros((KV_HEADS, ratio, rows_here), jnp.float32),
        jnp.zeros((KV_HEADS, ratio, rows_here, HEAD), jnp.float32),
    )
    local_rows = jnp.concatenate([past_kv, suffix_kv], axis=0)
    local_pos = jnp.concatenate([prefix_total + jnp.arange(past_slots, dtype=jnp.int32), query_pos])
    local_valid = jnp.concatenate(
        [jnp.arange(past_slots, dtype=jnp.int32) < past_count, jnp.ones((rows_here,), bool)]
    )
    state = absorb(state, query_heads, local_rows, local_pos, local_valid, query_pos, window)
    n_req = lax.axis_size(REQ)
    piece = lax.all_to_all(
        jnp.broadcast_to(prefix_kv[None], (n_req,) + prefix_kv.shape), REQ, 0, 0, tiled=False
    ).reshape(prefix_total, prefix_kv.shape[1])
    count = piece.shape[0]
    positions = jnp.arange(count, dtype=jnp.int32)
    maxima, totals, sums = absorb(
        state, query_heads, piece, positions, jnp.ones((count,), bool), query_pos, window
    )
    attended = (
        (sums / totals[..., None])
        .transpose(2, 0, 1, 3)
        .reshape(rows_here, HEADS * HEAD)
        .astype(jnp.bfloat16)
    )
    pair = jnp.concatenate([out_weight, lax.ppermute(out_weight, "x_lo", [(0, 1), (1, 0)])])
    n_z = lax.axis_size("z")
    block = pair.shape[0]
    halves = attended.reshape(rows_here, n_z, 2, out_weight.shape[0])
    halves = jnp.where(lax.axis_index("x_lo") == 0, halves, halves[:, :, ::-1])
    columns = lax.all_to_all(
        halves.reshape(rows_here, n_z, block), "z", 1, 0, tiled=False
    ).reshape(n_z * rows_here, block)
    partial = jnp.dot(columns, pair, preferred_element_type=jnp.float32).astype(jnp.bfloat16)
    returned = lax.all_to_all(
        partial.reshape(n_z, rows_here, partial.shape[1]), "z", 0, 0, tiled=False
    )
    projected = jnp.sum(returned.astype(jnp.float32), axis=0)
    mixed = layer_input.astype(jnp.float32) + projected
    scale = lax.rsqrt(jnp.mean(mixed * mixed, axis=-1, keepdims=True) + 1e-05)
    normed = (mixed * scale * norm_gain.astype(jnp.float32)).astype(jnp.bfloat16)
    swap = [(0, 1), (1, 0)]
    gate_both = jnp.concatenate([gate_weight, lax.ppermute(gate_weight, "core", swap)], axis=1)
    up_both = jnp.concatenate([up_weight, lax.ppermute(up_weight, "core", swap)], axis=1)
    down_both = jnp.concatenate([down_weight, lax.ppermute(down_weight, "core", swap)], axis=0)
    feed_axes = ("x_hi", "y")
    n_feed = lax.axis_size(feed_axes)
    chunks = 2
    size = rows_here // chunks
    feeds = []
    for c in range(chunks):
        rows = normed[c * size : (c + 1) * size]
        gathered = lax.all_to_all(
            jnp.broadcast_to(rows[None], (n_feed,) + rows.shape), feed_axes, 0, 0, tiled=False
        ).reshape(n_feed * size, rows.shape[1])
        gate = jnp.dot(gathered, gate_both, preferred_element_type=jnp.float32)
        upper = jnp.dot(gathered, up_both, preferred_element_type=jnp.float32)
        hidden = (jax.nn.silu(gate) * upper).astype(jnp.bfloat16)
        parts = jnp.dot(hidden, down_both, preferred_element_type=jnp.float32).astype(jnp.bfloat16)
        parts = lax.all_to_all(
            parts.reshape(n_feed, size, parts.shape[1]), feed_axes, 0, 0, tiled=False
        )
        feeds.append(jnp.sum(parts.astype(jnp.float32), axis=0))
    feed = jnp.concatenate(feeds, axis=0)
    live = offsets < suffix_len[0]
    return jnp.where(live[:, None], mixed + feed, 0.0).astype(jnp.bfloat16)


def solution(mesh):
    sizes = [mesh.shape["group"] // 2, 2, 2, mesh.shape["req"] // 4, 2]
    fine = jax.sharding.Mesh(mesh.devices.reshape(sizes), ALL)
    in_specs = (
        P(ALL, None),
        P(ALL, None),
        P(ALL, None),
        P(ALL, None),
        P(ALL, None),
        P(ALL),
        P(ALL),
        P(GROUP, None),
        P(),
        P(None, REQ),
        P(None, REQ),
        P(REQ, None),
    )
    out_specs = P(ALL, None)
    return jax.shard_map(shards, mesh=fine, in_specs=in_specs, out_specs=out_specs, check_vma=False)
```

```python
import jax
import jax.numpy as jnp
from jax import lax
from jax.sharding import PartitionSpec as P

HEADS = 24
KV_HEADS = 8
HEAD = 128
SINK = 4
GROUP = ("z", "x_lo")
REQ = ("x_hi", "y", "core")
ALL = GROUP + REQ


def absorb(state, query_heads, key_rows, key_pos, key_valid, query_pos, window):
    maxima, totals, sums = state
    count = key_rows.shape[0]
    key_heads = key_rows[:, : KV_HEADS * HEAD].reshape(count, KV_HEADS, HEAD)
    value_heads = key_rows[:, KV_HEADS * HEAD :].reshape(count, KV_HEADS, HEAD)
    scores = jnp.einsum(
        "skgh,nkh->kgsn", query_heads, key_heads, preferred_element_type=jnp.float32
    ) * HEAD ** (-0.5)
    near = query_pos[:, None] - key_pos[None, :] < window
    allowed = (
        key_valid[None, :]
        & (key_pos[None, :] <= query_pos[:, None])
        & ((key_pos[None, :] < SINK) | near)
    )
    scores = jnp.where(allowed, scores, -1e30)
    new_max = jnp.maximum(maxima, jnp.max(scores, axis=-1))
    expo = jnp.where(allowed, jnp.exp(scores - new_max[..., None]), 0.0)
    factor = jnp.exp(maxima - new_max)
    totals = totals * factor + jnp.sum(expo, axis=-1)
    sums = sums * factor[..., None] + jnp.einsum(
        "kgsn,nkh->kgsh", expo.astype(jnp.bfloat16), value_heads, preferred_element_type=jnp.float32
    )
    return (new_max, totals, sums)


def shards(
    layer_input,
    queries,
    suffix_kv,
    past_kv,
    prefix_kv,
    suffix_len,
    past_len,
    out_weight,
    norm_gain,
    gate_weight,
    up_weight,
    down_weight,
):
    rows_here = queries.shape[0]
    past_slots = past_kv.shape[0]
    prefix_total = prefix_kv.shape[0] * lax.axis_size(REQ)
    window = prefix_total + past_slots // 2
    past_count = past_len[0]
    offsets = jnp.arange(rows_here, dtype=jnp.int32)
    query_pos = prefix_total + past_count + offsets
    ratio = HEADS // KV_HEADS
    query_heads = queries.reshape(rows_here, KV_HEADS, ratio, HEAD)
    state = (
        jnp.full((KV_HEADS, ratio, rows_here), -1e30, jnp.float32),
        jnp.zeros((KV_HEADS, ratio, rows_here), jnp.float32),
        jnp.zeros((KV_HEADS, ratio, rows_here, HEAD), jnp.float32),
    )
    local_rows = jnp.concatenate([past_kv, suffix_kv], axis=0)
    local_pos = jnp.concatenate([prefix_total + jnp.arange(past_slots, dtype=jnp.int32), query_pos])
    local_valid = jnp.concatenate(
        [jnp.arange(past_slots, dtype=jnp.int32) < past_count, jnp.ones((rows_here,), bool)]
    )
    state = absorb(state, query_heads, local_rows, local_pos, local_valid, query_pos, window)
    n_req = lax.axis_size(REQ)
    piece = lax.all_to_all(
        jnp.broadcast_to(prefix_kv[None], (n_req,) + prefix_kv.shape), REQ, 0, 0, tiled=False
    ).reshape(prefix_total, prefix_kv.shape[1])
    count = piece.shape[0]
    positions = jnp.arange(count, dtype=jnp.int32)
    maxima, totals, sums = absorb(
        state, query_heads, piece, positions, jnp.ones((count,), bool), query_pos, window
    )
    attended = (
        (sums / totals[..., None])
        .transpose(2, 0, 1, 3)
        .reshape(rows_here, HEADS * HEAD)
        .astype(jnp.bfloat16)
    )
    swap = [(0, 1), (1, 0)]
    core = lax.axis_index("core")
    width = out_weight.shape[0] // 2
    fetched = lax.ppermute(
        lax.dynamic_slice_in_dim(out_weight, core * width, width, 0), "x_lo", swap
    )
    pair = jnp.concatenate([out_weight, fetched, lax.ppermute(fetched, "core", swap)])
    n_z = lax.axis_size("z")
    block = pair.shape[0]
    halves = attended.reshape(rows_here, n_z, 2, out_weight.shape[0])
    halves = jnp.where(lax.axis_index("x_lo") == 0, halves, halves[:, :, ::-1])
    other = halves[:, :, 1].reshape(rows_here, n_z, 2, width)
    other = jnp.where(core == 0, other, other[:, :, ::-1])
    ordered = jnp.concatenate(
        [halves[:, :, 0], other.reshape(rows_here, n_z, 2 * width)], axis=-1
    ).transpose(1, 0, 2)
    columns = lax.all_to_all(ordered, "z", 0, 0, tiled=False).reshape(n_z * rows_here, block)
    partial = jnp.dot(columns, pair, preferred_element_type=jnp.float32).astype(jnp.bfloat16)
    returned = lax.all_to_all(
        partial.reshape(n_z, rows_here, partial.shape[1]), "z", 0, 0, tiled=False
    )
    projected = jnp.sum(returned.astype(jnp.float32), axis=0)
    mixed = layer_input.astype(jnp.float32) + projected
    scale = lax.rsqrt(jnp.mean(mixed * mixed, axis=-1, keepdims=True) + 1e-05)
    normed = (mixed * scale * norm_gain.astype(jnp.float32)).astype(jnp.bfloat16)
    gate_both = jnp.concatenate([gate_weight, lax.ppermute(gate_weight, "core", swap)], axis=1)
    up_both = jnp.concatenate([up_weight, lax.ppermute(up_weight, "core", swap)], axis=1)
    down_both = jnp.concatenate([down_weight, lax.ppermute(down_weight, "core", swap)], axis=0)
    feed_axes = ("x_hi", "y")
    n_feed = lax.axis_size(feed_axes)
    chunks = 2
    size = rows_here // chunks
    feeds = []
    for c in range(chunks):
        rows = normed[c * size : (c + 1) * size]
        gathered = lax.all_to_all(
            jnp.broadcast_to(rows[None], (n_feed,) + rows.shape), feed_axes, 0, 0, tiled=False
        ).reshape(n_feed * size, rows.shape[1])
        gate = jnp.dot(gathered, gate_both, preferred_element_type=jnp.float32)
        upper = jnp.dot(gathered, up_both, preferred_element_type=jnp.float32)
        hidden = (jax.nn.silu(gate) * upper).astype(jnp.bfloat16)
        parts = jnp.dot(hidden, down_both, preferred_element_type=jnp.float32).astype(jnp.bfloat16)
        parts = lax.all_to_all(
            parts.reshape(n_feed, size, parts.shape[1]), feed_axes, 0, 0, tiled=False
        )
        feeds.append(jnp.sum(parts.astype(jnp.float32), axis=0))
    feed = jnp.concatenate(feeds, axis=0)
    live = offsets < suffix_len[0]
    return jnp.where(live[:, None], mixed + feed, 0.0).astype(jnp.bfloat16)


def solution(mesh):
    sizes = [mesh.shape["group"] // 2, 2, 2, mesh.shape["req"] // 4, 2]
    fine = jax.sharding.Mesh(mesh.devices.reshape(sizes), ALL)
    in_specs = (
        P(ALL, None),
        P(ALL, None),
        P(ALL, None),
        P(ALL, None),
        P(ALL, None),
        P(ALL),
        P(ALL),
        P(GROUP, None),
        P(),
        P(None, REQ),
        P(None, REQ),
        P(REQ, None),
    )
    out_specs = P(ALL, None)
    return jax.shard_map(shards, mesh=fine, in_specs=in_specs, out_specs=out_specs, check_vma=False)
```

```python
import jax
import jax.numpy as jnp
from jax import lax
from jax.sharding import PartitionSpec as P

HEADS = 24
KV_HEADS = 8
HEAD = 128
SINK = 4
GROUP = ("z", "x_lo")
REQ = ("x_hi", "y", "core")
ALL = GROUP + REQ


def absorb(state, query_heads, key_rows, key_pos, key_valid, query_pos, window):
    maxima, totals, sums = state
    count = key_rows.shape[0]
    key_heads = key_rows[:, : KV_HEADS * HEAD].reshape(count, KV_HEADS, HEAD)
    value_heads = key_rows[:, KV_HEADS * HEAD :].reshape(count, KV_HEADS, HEAD)
    scores = jnp.einsum(
        "skgh,nkh->kgsn", query_heads, key_heads, preferred_element_type=jnp.float32
    ) * HEAD ** (-0.5)
    near = query_pos[:, None] - key_pos[None, :] < window
    allowed = (
        key_valid[None, :]
        & (key_pos[None, :] <= query_pos[:, None])
        & ((key_pos[None, :] < SINK) | near)
    )
    scores = jnp.where(allowed, scores, -1e30)
    new_max = jnp.maximum(maxima, jnp.max(scores, axis=-1))
    expo = jnp.where(allowed, jnp.exp(scores - new_max[..., None]), 0.0)
    factor = jnp.exp(maxima - new_max)
    totals = totals * factor + jnp.sum(expo, axis=-1)
    sums = sums * factor[..., None] + jnp.einsum(
        "kgsn,nkh->kgsh", expo.astype(jnp.bfloat16), value_heads, preferred_element_type=jnp.float32
    )
    return (new_max, totals, sums)


def shards(
    layer_input,
    queries,
    suffix_kv,
    past_kv,
    prefix_kv,
    suffix_len,
    past_len,
    out_weight,
    norm_gain,
    gate_weight,
    up_weight,
    down_weight,
):
    rows_here = queries.shape[0]
    past_slots = past_kv.shape[0]
    prefix_total = prefix_kv.shape[0] * lax.axis_size(REQ)
    window = prefix_total + past_slots // 2
    past_count = past_len[0]
    offsets = jnp.arange(rows_here, dtype=jnp.int32)
    query_pos = prefix_total + past_count + offsets
    ratio = HEADS // KV_HEADS
    query_heads = queries.reshape(rows_here, KV_HEADS, ratio, HEAD)
    state = (
        jnp.full((KV_HEADS, ratio, rows_here), -1e30, jnp.float32),
        jnp.zeros((KV_HEADS, ratio, rows_here), jnp.float32),
        jnp.zeros((KV_HEADS, ratio, rows_here, HEAD), jnp.float32),
    )
    local_rows = jnp.concatenate([past_kv, suffix_kv], axis=0)
    local_pos = jnp.concatenate([prefix_total + jnp.arange(past_slots, dtype=jnp.int32), query_pos])
    local_valid = jnp.concatenate(
        [jnp.arange(past_slots, dtype=jnp.int32) < past_count, jnp.ones((rows_here,), bool)]
    )
    state = absorb(state, query_heads, local_rows, local_pos, local_valid, query_pos, window)
    n_req = lax.axis_size(REQ)
    piece = lax.all_to_all(
        jnp.broadcast_to(prefix_kv[None], (n_req,) + prefix_kv.shape), REQ, 0, 0, tiled=False
    ).reshape(prefix_total, prefix_kv.shape[1])
    count = piece.shape[0]
    positions = jnp.arange(count, dtype=jnp.int32)
    maxima, totals, sums = absorb(
        state, query_heads, piece, positions, jnp.ones((count,), bool), query_pos, window
    )
    attended = (
        (sums / totals[..., None])
        .transpose(2, 0, 1, 3)
        .reshape(rows_here, HEADS * HEAD)
        .astype(jnp.bfloat16)
    )
    swap = [(0, 1), (1, 0)]
    core = lax.axis_index("core")
    width = out_weight.shape[0] // 2
    fetched = lax.ppermute(
        lax.dynamic_slice_in_dim(out_weight, core * width, width, 0), "x_lo", swap
    )
    pair = jnp.concatenate([out_weight, fetched, lax.ppermute(fetched, "core", swap)])
    n_z = lax.axis_size("z")
    block = pair.shape[0]
    halves = attended.reshape(rows_here, n_z, 2, out_weight.shape[0])
    halves = jnp.where(lax.axis_index("x_lo") == 0, halves, halves[:, :, ::-1])
    other = halves[:, :, 1].reshape(rows_here, n_z, 2, width)
    other = jnp.where(core == 0, other, other[:, :, ::-1])
    ordered = jnp.concatenate(
        [halves[:, :, 0], other.reshape(rows_here, n_z, 2 * width)], axis=-1
    ).transpose(1, 0, 2)
    z = lax.axis_index("z")
    received = [jnp.take(ordered, z, axis=0)]
    for shift in range(1, n_z):
        received.append(
            lax.ppermute(
                jnp.take(ordered, (z + shift) % n_z, axis=0),
                "z",
                [(i, (i + shift) % n_z) for i in range(n_z)],
            )
        )
    sources = (z - jnp.arange(n_z, dtype=jnp.int32)) % n_z
    columns = jnp.take(jnp.stack(received), sources, axis=0).reshape(n_z * rows_here, block)
    partial = jnp.dot(columns, pair, preferred_element_type=jnp.float32).astype(jnp.bfloat16)
    returned = lax.all_to_all(
        partial.reshape(n_z, rows_here, partial.shape[1]), "z", 0, 0, tiled=False
    )
    projected = jnp.sum(returned.astype(jnp.float32), axis=0)
    mixed = layer_input.astype(jnp.float32) + projected
    scale = lax.rsqrt(jnp.mean(mixed * mixed, axis=-1, keepdims=True) + 1e-05)
    normed = (mixed * scale * norm_gain.astype(jnp.float32)).astype(jnp.bfloat16)
    gate_both = jnp.concatenate([gate_weight, lax.ppermute(gate_weight, "core", swap)], axis=1)
    up_both = jnp.concatenate([up_weight, lax.ppermute(up_weight, "core", swap)], axis=1)
    down_both = jnp.concatenate([down_weight, lax.ppermute(down_weight, "core", swap)], axis=0)
    feed_axes = ("x_hi", "y")
    n_feed = lax.axis_size(feed_axes)
    chunks = 2
    size = rows_here // chunks
    feeds = []
    for c in range(chunks):
        rows = normed[c * size : (c + 1) * size]
        gathered = lax.all_to_all(
            jnp.broadcast_to(rows[None], (n_feed,) + rows.shape), feed_axes, 0, 0, tiled=False
        ).reshape(n_feed * size, rows.shape[1])
        gate = jnp.dot(gathered, gate_both, preferred_element_type=jnp.float32)
        upper = jnp.dot(gathered, up_both, preferred_element_type=jnp.float32)
        hidden = (jax.nn.silu(gate) * upper).astype(jnp.bfloat16)
        parts = jnp.dot(hidden, down_both, preferred_element_type=jnp.float32).astype(jnp.bfloat16)
        parts = lax.all_to_all(
            parts.reshape(n_feed, size, parts.shape[1]), feed_axes, 0, 0, tiled=False
        )
        feeds.append(jnp.sum(parts.astype(jnp.float32), axis=0))
    feed = jnp.concatenate(feeds, axis=0)
    live = offsets < suffix_len[0]
    return jnp.where(live[:, None], mixed + feed, 0.0).astype(jnp.bfloat16)


def solution(mesh):
    sizes = [mesh.shape["group"] // 2, 2, 2, mesh.shape["req"] // 4, 2]
    fine = jax.sharding.Mesh(mesh.devices.reshape(sizes), ALL)
    in_specs = (
        P(ALL, None),
        P(ALL, None),
        P(ALL, None),
        P(ALL, None),
        P(ALL, None),
        P(ALL),
        P(ALL),
        P(GROUP, None),
        P(),
        P(None, REQ),
        P(None, REQ),
        P(REQ, None),
    )
    out_specs = P(ALL, None)
    return jax.shard_map(shards, mesh=fine, in_specs=in_specs, out_specs=out_specs, check_vma=False)
```

```python
import jax
import jax.numpy as jnp
from jax import lax
from jax.sharding import PartitionSpec as P

HEADS = 24
KV_HEADS = 8
HEAD = 128
SINK = 4
GROUP = ("z", "x_lo")
REQ = ("x_hi", "y", "core")
ALL = GROUP + REQ


def absorb(state, query_heads, key_rows, key_pos, key_valid, query_pos, window):
    maxima, totals, sums = state
    count = key_rows.shape[0]
    key_heads = key_rows[:, : KV_HEADS * HEAD].reshape(count, KV_HEADS, HEAD)
    value_heads = key_rows[:, KV_HEADS * HEAD :].reshape(count, KV_HEADS, HEAD)
    scores = jnp.einsum(
        "skgh,nkh->kgsn", query_heads, key_heads, preferred_element_type=jnp.float32
    ) * HEAD ** (-0.5)
    near = query_pos[:, None] - key_pos[None, :] < window
    allowed = (
        key_valid[None, :]
        & (key_pos[None, :] <= query_pos[:, None])
        & ((key_pos[None, :] < SINK) | near)
    )
    scores = jnp.where(allowed, scores, -1e30)
    new_max = jnp.maximum(maxima, jnp.max(scores, axis=-1))
    expo = jnp.where(allowed, jnp.exp(scores - new_max[..., None]), 0.0)
    factor = jnp.exp(maxima - new_max)
    totals = totals * factor + jnp.sum(expo, axis=-1)
    sums = sums * factor[..., None] + jnp.einsum(
        "kgsn,nkh->kgsh", expo.astype(jnp.bfloat16), value_heads, preferred_element_type=jnp.float32
    )
    return (new_max, totals, sums)


def shards(
    layer_input,
    queries,
    suffix_kv,
    past_kv,
    prefix_kv,
    suffix_len,
    past_len,
    out_weight,
    norm_gain,
    gate_weight,
    up_weight,
    down_weight,
):
    rows_here = queries.shape[0]
    past_slots = past_kv.shape[0]
    prefix_total = prefix_kv.shape[0] * lax.axis_size(REQ)
    window = prefix_total + past_slots // 2
    past_count = past_len[0]
    offsets = jnp.arange(rows_here, dtype=jnp.int32)
    query_pos = prefix_total + past_count + offsets
    ratio = HEADS // KV_HEADS
    query_heads = queries.reshape(rows_here, KV_HEADS, ratio, HEAD)
    state = (
        jnp.full((KV_HEADS, ratio, rows_here), -1e30, jnp.float32),
        jnp.zeros((KV_HEADS, ratio, rows_here), jnp.float32),
        jnp.zeros((KV_HEADS, ratio, rows_here, HEAD), jnp.float32),
    )
    local_rows = jnp.concatenate([past_kv, suffix_kv], axis=0)
    local_pos = jnp.concatenate([prefix_total + jnp.arange(past_slots, dtype=jnp.int32), query_pos])
    local_valid = jnp.concatenate(
        [jnp.arange(past_slots, dtype=jnp.int32) < past_count, jnp.ones((rows_here,), bool)]
    )
    state = absorb(state, query_heads, local_rows, local_pos, local_valid, query_pos, window)
    n_req = lax.axis_size(REQ)
    piece = lax.all_to_all(
        jnp.broadcast_to(prefix_kv[None], (n_req,) + prefix_kv.shape), REQ, 0, 0, tiled=False
    ).reshape(prefix_total, prefix_kv.shape[1])
    count = piece.shape[0]
    positions = jnp.arange(count, dtype=jnp.int32)
    maxima, totals, sums = absorb(
        state, query_heads, piece, positions, jnp.ones((count,), bool), query_pos, window
    )
    attended = (
        (sums / totals[..., None])
        .transpose(2, 0, 1, 3)
        .reshape(rows_here, HEADS * HEAD)
        .astype(jnp.bfloat16)
    )
    swap = [(0, 1), (1, 0)]
    core = lax.axis_index("core")
    width = out_weight.shape[0] // 2
    fetched = lax.ppermute(
        lax.dynamic_slice_in_dim(out_weight, core * width, width, 0), "x_lo", swap
    )
    pair = jnp.concatenate([out_weight, fetched, lax.ppermute(fetched, "core", swap)])
    n_z = lax.axis_size("z")
    block = pair.shape[0]
    halves = attended.reshape(rows_here, n_z, 2, out_weight.shape[0])
    halves = jnp.where(lax.axis_index("x_lo") == 0, halves, halves[:, :, ::-1])
    other = halves[:, :, 1].reshape(rows_here, n_z, 2, width)
    other = jnp.where(core == 0, other, other[:, :, ::-1])
    ordered = jnp.concatenate(
        [halves[:, :, 0], other.reshape(rows_here, n_z, 2 * width)], axis=-1
    ).transpose(1, 0, 2)
    columns = lax.all_to_all(ordered, "z", 0, 0, tiled=False).reshape(n_z * rows_here, block)
    partial = jnp.dot(columns, pair, preferred_element_type=jnp.float32).astype(jnp.bfloat16)
    returned = lax.all_to_all(
        partial.reshape(n_z, rows_here, partial.shape[1]), "z", 0, 0, tiled=False
    )
    projected = jnp.sum(returned.astype(jnp.float32), axis=0)
    mixed = layer_input.astype(jnp.float32) + projected
    scale = lax.rsqrt(jnp.mean(mixed * mixed, axis=-1, keepdims=True) + 1e-05)
    normed = (mixed * scale * norm_gain.astype(jnp.float32)).astype(jnp.bfloat16)
    weights = [
        (gate_weight, up_weight, down_weight),
        tuple(lax.ppermute(w, "core", swap) for w in (gate_weight, up_weight, down_weight)),
    ]
    feed_axes = ("x_hi", "y")
    n_feed = lax.axis_size(feed_axes)
    chunks = 2
    size = rows_here // chunks
    feeds = []
    for c in range(chunks):
        rows = normed[c * size : (c + 1) * size]
        gathered = lax.all_to_all(
            jnp.broadcast_to(rows[None], (n_feed,) + rows.shape), feed_axes, 0, 0, tiled=False
        ).reshape(n_feed * size, rows.shape[1])
        parts = 0.0
        for gate_w, up_w, down_w in weights:
            gate = jnp.dot(gathered, gate_w, preferred_element_type=jnp.float32)
            upper = jnp.dot(gathered, up_w, preferred_element_type=jnp.float32)
            hidden = (jax.nn.silu(gate) * upper).astype(jnp.bfloat16)
            parts = parts + jnp.dot(hidden, down_w, preferred_element_type=jnp.float32)
        parts = parts.astype(jnp.bfloat16)
        parts = lax.all_to_all(
            parts.reshape(n_feed, size, parts.shape[1]), feed_axes, 0, 0, tiled=False
        )
        feeds.append(jnp.sum(parts.astype(jnp.float32), axis=0))
    feed = jnp.concatenate(feeds, axis=0)
    live = offsets < suffix_len[0]
    return jnp.where(live[:, None], mixed + feed, 0.0).astype(jnp.bfloat16)


def solution(mesh):
    sizes = [mesh.shape["group"] // 2, 2, 2, mesh.shape["req"] // 4, 2]
    fine = jax.sharding.Mesh(mesh.devices.reshape(sizes), ALL)
    in_specs = (
        P(ALL, None),
        P(ALL, None),
        P(ALL, None),
        P(ALL, None),
        P(ALL, None),
        P(ALL),
        P(ALL),
        P(GROUP, None),
        P(),
        P(None, REQ),
        P(None, REQ),
        P(REQ, None),
    )
    out_specs = P(ALL, None)
    return jax.shard_map(shards, mesh=fine, in_specs=in_specs, out_specs=out_specs, check_vma=False)
```

```python
import jax
import jax.numpy as jnp
from jax import lax
from jax.sharding import PartitionSpec as P

HEADS = 24
KV_HEADS = 8
HEAD = 128
SINK = 4
GROUP = ("z", "x_lo")
REQ = ("x_hi", "y", "core")
ALL = GROUP + REQ


def absorb(state, query_heads, key_rows, key_pos, key_valid, query_pos, window):
    maxima, totals, sums = state
    count = key_rows.shape[0]
    key_heads = key_rows[:, : KV_HEADS * HEAD].reshape(count, KV_HEADS, HEAD)
    value_heads = key_rows[:, KV_HEADS * HEAD :].reshape(count, KV_HEADS, HEAD)
    scores = jnp.einsum(
        "skgh,nkh->kgsn", query_heads, key_heads, preferred_element_type=jnp.float32
    ) * HEAD ** (-0.5)
    near = query_pos[:, None] - key_pos[None, :] < window
    allowed = (
        key_valid[None, :]
        & (key_pos[None, :] <= query_pos[:, None])
        & ((key_pos[None, :] < SINK) | near)
    )
    scores = jnp.where(allowed, scores, -1e30)
    new_max = jnp.maximum(maxima, jnp.max(scores, axis=-1))
    expo = jnp.where(allowed, jnp.exp(scores - new_max[..., None]), 0.0)
    factor = jnp.exp(maxima - new_max)
    totals = totals * factor + jnp.sum(expo, axis=-1)
    sums = sums * factor[..., None] + jnp.einsum(
        "kgsn,nkh->kgsh", expo.astype(jnp.bfloat16), value_heads, preferred_element_type=jnp.float32
    )
    return (new_max, totals, sums)


def shards(
    layer_input,
    queries,
    suffix_kv,
    past_kv,
    prefix_kv,
    suffix_len,
    past_len,
    out_weight,
    norm_gain,
    gate_weight,
    up_weight,
    down_weight,
):
    rows_here = queries.shape[0]
    past_slots = past_kv.shape[0]
    prefix_total = prefix_kv.shape[0] * lax.axis_size(REQ)
    window = prefix_total + past_slots // 2
    past_count = past_len[0]
    offsets = jnp.arange(rows_here, dtype=jnp.int32)
    query_pos = prefix_total + past_count + offsets
    ratio = HEADS // KV_HEADS
    query_heads = queries.reshape(rows_here, KV_HEADS, ratio, HEAD)
    state = (
        jnp.full((KV_HEADS, ratio, rows_here), -1e30, jnp.float32),
        jnp.zeros((KV_HEADS, ratio, rows_here), jnp.float32),
        jnp.zeros((KV_HEADS, ratio, rows_here, HEAD), jnp.float32),
    )
    local_rows = jnp.concatenate([past_kv, suffix_kv], axis=0)
    local_pos = jnp.concatenate([prefix_total + jnp.arange(past_slots, dtype=jnp.int32), query_pos])
    local_valid = jnp.concatenate(
        [jnp.arange(past_slots, dtype=jnp.int32) < past_count, jnp.ones((rows_here,), bool)]
    )
    state = absorb(state, query_heads, local_rows, local_pos, local_valid, query_pos, window)
    n_req = lax.axis_size(REQ)
    piece = lax.all_to_all(
        jnp.broadcast_to(prefix_kv[None], (n_req,) + prefix_kv.shape), REQ, 0, 0, tiled=False
    ).reshape(prefix_total, prefix_kv.shape[1])
    count = piece.shape[0]
    positions = jnp.arange(count, dtype=jnp.int32)
    maxima, totals, sums = absorb(
        state, query_heads, piece, positions, jnp.ones((count,), bool), query_pos, window
    )
    attended = (
        (sums / totals[..., None])
        .transpose(2, 0, 1, 3)
        .reshape(rows_here, HEADS * HEAD)
        .astype(jnp.bfloat16)
    )
    swap = [(0, 1), (1, 0)]
    core = lax.axis_index("core")
    width = out_weight.shape[0] // 2
    fetched = lax.ppermute(
        lax.dynamic_slice_in_dim(out_weight, core * width, width, 0), "x_lo", swap
    )
    pair = jnp.concatenate([out_weight, fetched, lax.ppermute(fetched, "core", swap)])
    n_z = lax.axis_size("z")
    block = pair.shape[0]
    halves = attended.reshape(rows_here, n_z, 2, out_weight.shape[0])
    halves = jnp.where(lax.axis_index("x_lo") == 0, halves, halves[:, :, ::-1])
    other = halves[:, :, 1].reshape(rows_here, n_z, 2, width)
    other = jnp.where(core == 0, other, other[:, :, ::-1])
    ordered = jnp.concatenate(
        [halves[:, :, 0], other.reshape(rows_here, n_z, 2 * width)], axis=-1
    ).transpose(1, 0, 2)
    columns = lax.all_to_all(ordered, "z", 0, 0, tiled=False).reshape(n_z * rows_here, block)
    partial = jnp.dot(columns, pair, preferred_element_type=jnp.float32).astype(jnp.bfloat16)
    returned = lax.all_to_all(
        partial.reshape(n_z, rows_here, partial.shape[1]), "z", 0, 0, tiled=False
    )
    projected = jnp.sum(returned.astype(jnp.float32), axis=0)
    mixed = layer_input.astype(jnp.float32) + projected
    scale = lax.rsqrt(jnp.mean(mixed * mixed, axis=-1, keepdims=True) + 1e-05)
    normed = (mixed * scale * norm_gain.astype(jnp.float32)).astype(jnp.bfloat16)
    weights = [
        (gate_weight, up_weight, down_weight),
        tuple(lax.ppermute(w, "core", swap) for w in (gate_weight, up_weight, down_weight)),
    ]
    feed_axes = ("x_hi", "y")
    n_feed = lax.axis_size(feed_axes)
    edge = rows_here // 4
    bounds = [0, edge, rows_here - edge, rows_here]
    feeds = []
    for c in range(len(bounds) - 1):
        rows = normed[bounds[c] : bounds[c + 1]]
        size = rows.shape[0]
        gathered = lax.all_to_all(
            jnp.broadcast_to(rows[None], (n_feed,) + rows.shape), feed_axes, 0, 0, tiled=False
        ).reshape(n_feed * size, rows.shape[1])
        parts = 0.0
        for gate_w, up_w, down_w in weights:
            gate = jnp.dot(gathered, gate_w, preferred_element_type=jnp.float32)
            upper = jnp.dot(gathered, up_w, preferred_element_type=jnp.float32)
            hidden = (jax.nn.silu(gate) * upper).astype(jnp.bfloat16)
            parts = parts + jnp.dot(hidden, down_w, preferred_element_type=jnp.float32)
        parts = parts.astype(jnp.bfloat16)
        parts = lax.all_to_all(
            parts.reshape(n_feed, size, parts.shape[1]), feed_axes, 0, 0, tiled=False
        )
        feeds.append(jnp.sum(parts.astype(jnp.float32), axis=0))
    feed = jnp.concatenate(feeds, axis=0)
    live = offsets < suffix_len[0]
    return jnp.where(live[:, None], mixed + feed, 0.0).astype(jnp.bfloat16)


def solution(mesh):
    sizes = [mesh.shape["group"] // 2, 2, 2, mesh.shape["req"] // 4, 2]
    fine = jax.sharding.Mesh(mesh.devices.reshape(sizes), ALL)
    in_specs = (
        P(ALL, None),
        P(ALL, None),
        P(ALL, None),
        P(ALL, None),
        P(ALL, None),
        P(ALL),
        P(ALL),
        P(GROUP, None),
        P(),
        P(None, REQ),
        P(None, REQ),
        P(REQ, None),
    )
    out_specs = P(ALL, None)
    return jax.shard_map(shards, mesh=fine, in_specs=in_specs, out_specs=out_specs, check_vma=False)
```

```python
import jax
import jax.numpy as jnp
from jax import lax
from jax.sharding import PartitionSpec as P

HEADS = 24
KV_HEADS = 8
HEAD = 128
SINK = 4
GROUP = ("z", "x_lo")
REQ = ("x_hi", "y", "core")
ALL = GROUP + REQ


def absorb(state, query_heads, key_rows, key_pos, key_valid, query_pos, window):
    maxima, totals, sums = state
    count = key_rows.shape[0]
    key_heads = key_rows[:, : KV_HEADS * HEAD].reshape(count, KV_HEADS, HEAD)
    value_heads = key_rows[:, KV_HEADS * HEAD :].reshape(count, KV_HEADS, HEAD)
    scores = jnp.einsum(
        "skgh,nkh->kgsn", query_heads, key_heads, preferred_element_type=jnp.float32
    ) * HEAD ** (-0.5)
    near = query_pos[:, None] - key_pos[None, :] < window
    allowed = (
        key_valid[None, :]
        & (key_pos[None, :] <= query_pos[:, None])
        & ((key_pos[None, :] < SINK) | near)
    )
    scores = jnp.where(allowed, scores, -1e30)
    new_max = jnp.maximum(maxima, jnp.max(scores, axis=-1))
    expo = jnp.where(allowed, jnp.exp(scores - new_max[..., None]), 0.0)
    factor = jnp.exp(maxima - new_max)
    totals = totals * factor + jnp.sum(expo, axis=-1)
    sums = sums * factor[..., None] + jnp.einsum(
        "kgsn,nkh->kgsh", expo.astype(jnp.bfloat16), value_heads, preferred_element_type=jnp.float32
    )
    return (new_max, totals, sums)


def shards(
    layer_input,
    queries,
    suffix_kv,
    past_kv,
    prefix_kv,
    suffix_len,
    past_len,
    out_weight,
    norm_gain,
    gate_weight,
    up_weight,
    down_weight,
):
    rows_here = queries.shape[0]
    past_slots = past_kv.shape[0]
    prefix_total = prefix_kv.shape[0] * lax.axis_size(REQ)
    window = prefix_total + past_slots // 2
    past_count = past_len[0]
    offsets = jnp.arange(rows_here, dtype=jnp.int32)
    query_pos = prefix_total + past_count + offsets
    ratio = HEADS // KV_HEADS
    query_heads = queries.reshape(rows_here, KV_HEADS, ratio, HEAD)
    state = (
        jnp.full((KV_HEADS, ratio, rows_here), -1e30, jnp.float32),
        jnp.zeros((KV_HEADS, ratio, rows_here), jnp.float32),
        jnp.zeros((KV_HEADS, ratio, rows_here, HEAD), jnp.float32),
    )
    local_rows = jnp.concatenate([past_kv, suffix_kv], axis=0)
    local_pos = jnp.concatenate([prefix_total + jnp.arange(past_slots, dtype=jnp.int32), query_pos])
    local_valid = jnp.concatenate(
        [jnp.arange(past_slots, dtype=jnp.int32) < past_count, jnp.ones((rows_here,), bool)]
    )
    state = absorb(state, query_heads, local_rows, local_pos, local_valid, query_pos, window)
    n_req = lax.axis_size(REQ)
    piece = lax.all_to_all(
        jnp.broadcast_to(prefix_kv[None], (n_req,) + prefix_kv.shape), REQ, 0, 0, tiled=False
    ).reshape(prefix_total, prefix_kv.shape[1])
    count = piece.shape[0]
    positions = jnp.arange(count, dtype=jnp.int32)
    maxima, totals, sums = absorb(
        state, query_heads, piece, positions, jnp.ones((count,), bool), query_pos, window
    )
    attended = (
        (sums / totals[..., None])
        .transpose(2, 0, 1, 3)
        .reshape(rows_here, HEADS * HEAD)
        .astype(jnp.bfloat16)
    )
    swap = [(0, 1), (1, 0)]
    core = lax.axis_index("core")
    width = out_weight.shape[0] // 2
    fetched = lax.ppermute(
        lax.dynamic_slice_in_dim(out_weight, core * width, width, 0), "x_lo", swap
    )
    pair = jnp.concatenate([out_weight, fetched, lax.ppermute(fetched, "core", swap)])
    n_z = lax.axis_size("z")
    block = pair.shape[0]
    halves = attended.reshape(rows_here, n_z, 2, out_weight.shape[0])
    halves = jnp.where(lax.axis_index("x_lo") == 0, halves, halves[:, :, ::-1])
    other = halves[:, :, 1].reshape(rows_here, n_z, 2, width)
    other = jnp.where(core == 0, other, other[:, :, ::-1])
    ordered = jnp.concatenate(
        [halves[:, :, 0], other.reshape(rows_here, n_z, 2 * width)], axis=-1
    ).transpose(1, 0, 2)
    columns = lax.all_to_all(ordered, "z", 0, 0, tiled=False).reshape(n_z * rows_here, block)
    partial = jnp.dot(columns, pair, preferred_element_type=jnp.float32).astype(jnp.bfloat16)
    returned = lax.all_to_all(
        partial.reshape(n_z, rows_here, partial.shape[1]), "z", 0, 0, tiled=False
    )
    projected = jnp.sum(returned.astype(jnp.float32), axis=0)
    mixed = layer_input.astype(jnp.float32) + projected
    scale = lax.rsqrt(jnp.mean(mixed * mixed, axis=-1, keepdims=True) + 1e-05)
    normed = (mixed * scale * norm_gain.astype(jnp.float32)).astype(jnp.bfloat16)
    gate_both = lax.all_gather(gate_weight, "core", axis=1, tiled=True)
    up_both = lax.all_gather(up_weight, "core", axis=1, tiled=True)
    down_both = lax.all_gather(down_weight, "core", axis=0, tiled=True)
    feed_axes = ("x_hi", "y")
    n_feed = lax.axis_size(feed_axes)
    chunks = 2
    size = rows_here // chunks
    feeds = []
    for c in range(chunks):
        rows = normed[c * size : (c + 1) * size]
        gathered = lax.all_to_all(
            jnp.broadcast_to(rows[None], (n_feed,) + rows.shape), feed_axes, 0, 0, tiled=False
        ).reshape(n_feed * size, rows.shape[1])
        gate = jnp.dot(gathered, gate_both, preferred_element_type=jnp.float32)
        upper = jnp.dot(gathered, up_both, preferred_element_type=jnp.float32)
        hidden = (jax.nn.silu(gate) * upper).astype(jnp.bfloat16)
        parts = jnp.dot(hidden, down_both, preferred_element_type=jnp.float32).astype(jnp.bfloat16)
        parts = lax.all_to_all(
            parts.reshape(n_feed, size, parts.shape[1]), feed_axes, 0, 0, tiled=False
        )
        feeds.append(jnp.sum(parts.astype(jnp.float32), axis=0))
    feed = jnp.concatenate(feeds, axis=0)
    live = offsets < suffix_len[0]
    return jnp.where(live[:, None], mixed + feed, 0.0).astype(jnp.bfloat16)


def solution(mesh):
    sizes = [mesh.shape["group"] // 2, 2, 2, mesh.shape["req"] // 4, 2]
    fine = jax.sharding.Mesh(mesh.devices.reshape(sizes), ALL)
    in_specs = (
        P(ALL, None),
        P(ALL, None),
        P(ALL, None),
        P(ALL, None),
        P(ALL, None),
        P(ALL),
        P(ALL),
        P(GROUP, None),
        P(),
        P(None, REQ),
        P(None, REQ),
        P(REQ, None),
    )
    out_specs = P(ALL, None)
    return jax.shard_map(shards, mesh=fine, in_specs=in_specs, out_specs=out_specs, check_vma=False)
```

```python
import jax
import jax.numpy as jnp
from jax import lax
from jax.sharding import PartitionSpec as P

HEADS = 24
KV_HEADS = 8
HEAD = 128
SINK = 4
GROUP = ("z", "x_lo")
REQ = ("x_hi", "y", "core")
ALL = GROUP + REQ


def absorb(state, query_heads, key_rows, key_pos, key_valid, query_pos, window):
    maxima, totals, sums = state
    count = key_rows.shape[0]
    key_heads = key_rows[:, : KV_HEADS * HEAD].reshape(count, KV_HEADS, HEAD)
    value_heads = key_rows[:, KV_HEADS * HEAD :].reshape(count, KV_HEADS, HEAD)
    scores = jnp.einsum(
        "skgh,nkh->kgsn", query_heads, key_heads, preferred_element_type=jnp.float32
    ) * HEAD ** (-0.5)
    near = query_pos[:, None] - key_pos[None, :] < window
    allowed = (
        key_valid[None, :]
        & (key_pos[None, :] <= query_pos[:, None])
        & ((key_pos[None, :] < SINK) | near)
    )
    scores = jnp.where(allowed, scores, -1e30)
    new_max = jnp.maximum(maxima, jnp.max(scores, axis=-1))
    expo = jnp.where(allowed, jnp.exp(scores - new_max[..., None]), 0.0)
    factor = jnp.exp(maxima - new_max)
    totals = totals * factor + jnp.sum(expo, axis=-1)
    sums = sums * factor[..., None] + jnp.einsum(
        "kgsn,nkh->kgsh", expo.astype(jnp.bfloat16), value_heads, preferred_element_type=jnp.float32
    )
    return (new_max, totals, sums)


def shards(
    layer_input,
    queries,
    suffix_kv,
    past_kv,
    prefix_kv,
    suffix_len,
    past_len,
    out_weight,
    norm_gain,
    gate_weight,
    up_weight,
    down_weight,
):
    rows_here = queries.shape[0]
    past_slots = past_kv.shape[0]
    prefix_total = prefix_kv.shape[0] * lax.axis_size(REQ)
    window = prefix_total + past_slots // 2
    past_count = past_len[0]
    offsets = jnp.arange(rows_here, dtype=jnp.int32)
    query_pos = prefix_total + past_count + offsets
    ratio = HEADS // KV_HEADS
    query_heads = queries.reshape(rows_here, KV_HEADS, ratio, HEAD)
    state = (
        jnp.full((KV_HEADS, ratio, rows_here), -1e30, jnp.float32),
        jnp.zeros((KV_HEADS, ratio, rows_here), jnp.float32),
        jnp.zeros((KV_HEADS, ratio, rows_here, HEAD), jnp.float32),
    )
    local_rows = jnp.concatenate([past_kv, suffix_kv], axis=0)
    local_pos = jnp.concatenate([prefix_total + jnp.arange(past_slots, dtype=jnp.int32), query_pos])
    local_valid = jnp.concatenate(
        [jnp.arange(past_slots, dtype=jnp.int32) < past_count, jnp.ones((rows_here,), bool)]
    )
    state = absorb(state, query_heads, local_rows, local_pos, local_valid, query_pos, window)
    n_req = lax.axis_size(REQ)
    piece = lax.all_to_all(
        jnp.broadcast_to(prefix_kv[None], (n_req,) + prefix_kv.shape), REQ, 0, 0, tiled=False
    ).reshape(prefix_total, prefix_kv.shape[1])
    count = piece.shape[0]
    positions = jnp.arange(count, dtype=jnp.int32)
    _, totals, sums = absorb(
        state, query_heads, piece, positions, jnp.ones((count,), bool), query_pos, window
    )
    attended = (
        (sums / totals[..., None])
        .transpose(2, 0, 1, 3)
        .reshape(rows_here, HEADS * HEAD)
        .astype(jnp.bfloat16)
    )
    swap = [(0, 1), (1, 0)]
    core = lax.axis_index("core")
    width = out_weight.shape[0] // 2
    fetched = lax.ppermute(
        lax.dynamic_slice_in_dim(out_weight, core * width, width, 0), "x_lo", swap
    )
    pair = jnp.concatenate([out_weight, fetched, lax.ppermute(fetched, "core", swap)])
    n_z = lax.axis_size("z")
    block = pair.shape[0]
    halves = attended.reshape(rows_here, n_z, 2, out_weight.shape[0])
    halves = jnp.where(lax.axis_index("x_lo") == 0, halves, halves[:, :, ::-1])
    other = halves[:, :, 1].reshape(rows_here, n_z, 2, width)
    other = jnp.where(core == 0, other, other[:, :, ::-1])
    ordered = jnp.concatenate(
        [halves[:, :, 0], other.reshape(rows_here, n_z, 2 * width)], axis=-1
    ).transpose(1, 0, 2)
    columns = lax.all_to_all(ordered, "z", 0, 0, tiled=False)
    columns = columns.reshape(n_z * rows_here, block)
    partial = jnp.dot(columns, pair, preferred_element_type=jnp.float32).astype(jnp.bfloat16)
    returned = lax.all_to_all(
        partial.reshape(n_z, rows_here, partial.shape[1]), "z", 0, 0, tiled=False
    )
    projected = jnp.sum(returned.astype(jnp.float32), axis=0)
    mixed = layer_input.astype(jnp.float32) + projected
    scale = lax.rsqrt(jnp.mean(mixed * mixed, axis=-1, keepdims=True) + 1e-05)
    normed = (mixed * scale * norm_gain.astype(jnp.float32)).astype(jnp.bfloat16)
    weights = [
        (gate_weight, up_weight, down_weight),
        tuple(lax.ppermute(w, "core", swap) for w in (gate_weight, up_weight, down_weight)),
    ]
    feed_axes = ("x_hi", "y")
    n_feed = lax.axis_size(feed_axes)
    chunks = 2
    size = rows_here // chunks
    feeds = []
    for c in range(chunks):
        rows = normed[c * size : (c + 1) * size]
        gathered = lax.all_to_all(
            jnp.broadcast_to(rows[None], (n_feed,) + rows.shape), feed_axes, 0, 0, tiled=False
        ).reshape(n_feed * size, rows.shape[1])
        parts = 0.0
        for gate_w, up_w, down_w in weights:
            gate = jnp.dot(gathered, gate_w, preferred_element_type=jnp.float32)
            upper = jnp.dot(gathered, up_w, preferred_element_type=jnp.float32)
            hidden = (jax.nn.silu(gate) * upper).astype(jnp.bfloat16)
            parts = parts + jnp.dot(hidden, down_w, preferred_element_type=jnp.float32)
        parts = parts.astype(jnp.bfloat16)
        parts = lax.all_to_all(
            parts.reshape(n_feed, size, parts.shape[1]), feed_axes, 0, 0, tiled=False
        )
        feeds.append(jnp.sum(parts.astype(jnp.float32), axis=0))
    feed = jnp.concatenate(feeds, axis=0)
    live = offsets < suffix_len[0]
    return jnp.where(live[:, None], mixed + feed, 0.0).astype(jnp.bfloat16)


def solution(mesh):
    sizes = [mesh.shape["group"] // 2, 2, 2, mesh.shape["req"] // 4, 2]
    fine = jax.sharding.Mesh(mesh.devices.reshape(sizes), ALL)
    in_specs = (
        P(ALL, None),
        P(ALL, None),
        P(ALL, None),
        P(ALL, None),
        P(ALL, None),
        P(ALL),
        P(ALL),
        P(GROUP, None),
        P(),
        P(None, REQ),
        P(None, REQ),
        P(REQ, None),
    )
    out_specs = P(ALL, None)

    return jax.shard_map(shards, mesh=fine, in_specs=in_specs, out_specs=out_specs, check_vma=False)
```
